256 devices in a mesh: space: 128 (over z_lo, y, x, core), op: 2 (over z_hi).
Axes of the slice: x: 4, y: 4, z: 8 (z_hi: 2, z_lo: 4; z = z_hi * 4 + z_lo), core: 2. Of those that a mesh axis runs over, the one named last changes fastest.
Arguments:
- order_field: float32 [16, 1024, 64, 128], P('op', 'space'), may hold values from 0 to 1
- adjoint_next: float32 [16, 1024, 64, 128], P('op', 'space'), may hold values from -6 to 6
- mobility: float32 [16], P('op'), may hold values from 0.5 to 2
- labels: int32 [1024, 128], P('space'), may hold values from 0 to 15
Outputs:
- order_next: float32 [16, 1024, 64, 128], P('op', 'space')
- adjoint_order: float32 [16, 1024, 64, 128], P('op', 'space')
The draws below stay inside these ranges and needn't reach their ends.
All inputs are finite; a program needn't handle non-finite values.
Results may differ from the reference program's by a relative error of at most 0.00002.
Values sent between devices are 32-bit elements; how exact they have to be, the bound alone decides.
No kernel may reach another device: no remote copies, remote signals or barrier semaphores. Data moves between devices by JAX's collectives and lax.ppermute only.
A program may use at most 128 MiB of HBM per device.

```python
import math
import jax
import jax.numpy as jnp

P_SIZE = 16
NY = 128
NZ = 64
NX = 1024


def place_ends(drawn, key, least, top_value):
    shape = drawn.shape
    index_at = [jax.random.randint(jax.random.fold_in(key, axis), (), 0, shape[axis]) for axis in range(len(shape))]
    drawn = drawn.at[tuple(index_at)].set(least)
    longest = shape.index(max(shape))
    index_at[longest] = (index_at[longest] + 1) % shape[longest]
    return drawn.at[tuple(index_at)].set(top_value)


def steps_of(rng, dims, split, least, largest):
    gain, own = 1.0, jax.random.fold_in(rng, 6)
    for axis_at, shards_of in split:
        steps = jnp.exp(jax.random.uniform(jax.random.fold_in(own, axis_at), (shards_of,), jnp.float32, least / len(split), largest / len(split)))
        gain = gain * jnp.repeat(steps, dims[axis_at] // shards_of).reshape([-1 if axis == axis_at else 1 for axis in range(len(dims))])
    return gain


def scatter_about(stream_key, extent, scale, reach, shards=(), kind=jnp.bfloat16):
    values = scale * jax.random.normal(stream_key, extent, jnp.float32)
    if shards:
        values = values * steps_of(stream_key, extent, shards, -0.22, 0.18)
    return jnp.clip(values, -reach, reach).astype(kind)


def setup_inputs(seed: int = 0) -> dict:
    key_list = jax.random.split(jax.random.key(seed), 5)
    order_field = jnp.clip(1.0 * jax.random.uniform(key_list[0], (P_SIZE, NX, NZ, NY), jnp.float32) ** steps_of(key_list[0], (P_SIZE, NX, NZ, NY), ((0, 2), (1, 128)), -0.2, 0.2), 0.0, 1.0)
    adjoint_next = scatter_about(key_list[1], (P_SIZE, NX, NZ, NY), 1.0, 6.0, ((0, 2), (1, 128)), jnp.float32)
    mobility = jnp.clip(jnp.exp(math.log(2.0) - 1.3862944 * jax.random.uniform(key_list[2], (P_SIZE,), jnp.float32) ** steps_of(key_list[2], (P_SIZE,), ((0, 2),), -0.2, 0.2)), 0.5, 2.0)
    labels = place_ends(jax.random.randint(key_list[3], (NX, NY), 0, P_SIZE), jax.random.fold_in(key_list[3], 1), 0, P_SIZE - 1).astype(jnp.int32)
    return dict(order_field=order_field, adjoint_next=adjoint_next, mobility=mobility, labels=labels)


def laplace(field):
    beside = jnp.roll(field, 1, 1) + jnp.roll(field, -1, 1)
    beside = beside + jnp.roll(field, 1, 3) + jnp.roll(field, -1, 3)
    upper = jnp.concatenate([field[:, :, 1:], field[:, :, -1:]], axis=2)
    lower = jnp.concatenate([field[:, :, :1], field[:, :, :-1]], axis=2)
    return beside + upper + lower - 6.0 * field


def reference(order_field, adjoint_next, mobility, labels):
    indices = jnp.arange(P_SIZE, dtype=jnp.int32)
    foreign = (labels[None, :, None, :] != indices[:, None, None, None]).astype(jnp.float32)
    rates = mobility[:, None, None, None]
    squares = jnp.sum(order_field * order_field, axis=0)
    potential = (-1.0 + 2.0 * foreign) * order_field - 2.0 * order_field ** 3 + 3.0 * order_field * squares - 0.5 * laplace(order_field)
    order_next = order_field - 0.1 * rates * potential
    weighted = 0.1 * rates * adjoint_next
    coupled = jnp.sum(order_field * weighted, axis=0)
    local_part = (-1.0 + 2.0 * foreign - 6.0 * order_field * order_field + 3.0 * squares) * weighted
    adjoint_order = adjoint_next - (local_part + 6.0 * order_field * coupled - 0.5 * laplace(weighted))
    return order_next, adjoint_order
```

```python
import jax
import jax.numpy as jnp
from jax import lax
from jax.sharding import PartitionSpec as P


def extended(cells, sides, width):
    for axis, dim in sides:
        count = lax.axis_size(axis)
        head = lax.slice_in_dim(cells, 0, width, axis=dim)
        tail = lax.slice_in_dim(cells, cells.shape[dim] - width, cells.shape[dim], axis=dim)
        cells = jnp.concatenate(
            [
                lax.ppermute(tail, axis, [(i, (i + 1) % count) for i in range(count)]),
                cells,
                lax.ppermute(head, axis, [((i + 1) % count, i) for i in range(count)]),
            ],
            axis=dim,
        )
    return cells


def laplace(padded):
    centre = padded[:, 1:-1]
    beside = padded[:, 2:] + padded[:, :-2]
    beside = beside + jnp.roll(centre, 1, 3) + jnp.roll(centre, -1, 3)
    upper = jnp.concatenate([centre[:, :, 1:], centre[:, :, -1:]], axis=2)
    lower = jnp.concatenate([centre[:, :, :1], centre[:, :, :-1]], axis=2)
    return beside + upper + lower - 6.0 * centre


def local(order_field, adjoint_next, mobility, labels):
    local_count = order_field.shape[0]
    first = lax.axis_index("op") * local_count
    indices = first + jnp.arange(local_count, dtype=jnp.int32)
    foreign = (labels[None, :, None, :] != indices[:, None, None, None]).astype(jnp.float32)
    rates = mobility[:, None, None, None]
    weighted = 0.1 * rates * adjoint_next
    partial = jnp.stack([jnp.sum(order_field * order_field, axis=0), jnp.sum(order_field * weighted, axis=0)])
    count = lax.axis_size("op")
    other = lax.ppermute(partial, "op", [(i, (i + 1) % count) for i in range(count)])
    total = partial + other
    squares, coupled = total[0], total[1]
    padded_state = extended(order_field, (("space", 1),), 1)
    padded_weight = extended(weighted, (("space", 1),), 1)
    potential = (
        (-1.0 + 2.0 * foreign) * order_field
        - 2.0 * order_field**3
        + 3.0 * order_field * squares
        - 0.5 * laplace(padded_state)
    )
    order_next = order_field - 0.1 * rates * potential
    local_part = (-1.0 + 2.0 * foreign - 6.0 * order_field * order_field + 3.0 * squares) * weighted
    adjoint_order = adjoint_next - (
        local_part + 6.0 * order_field * coupled - 0.5 * laplace(padded_weight)
    )
    return (order_next, adjoint_order)


def solution(mesh):
    placed = (P("op", "space", None, None), P("op", "space", None, None), P("op"), P("space", None))
    return jax.shard_map(
        local,
        mesh=mesh,
        in_specs=placed,
        out_specs=(P("op", "space", None, None), P("op", "space", None, None)),
        check_vma=False,
    )
```

```python
import jax
import jax.numpy as jnp
from jax import lax
from jax.experimental import pallas as pl
from jax.experimental.pallas import tpu as pltpu
from jax.sharding import PartitionSpec as P


def neighbour_rows(cells, axis):
    count = lax.axis_size(axis)
    head = cells[:, :1]
    tail = cells[:, -1:]
    below = lax.ppermute(tail, axis, [(i, (i + 1) % count) for i in range(count)])
    above = lax.ppermute(head, axis, [((i + 1) % count, i) for i in range(count)])
    return jnp.concatenate([below, above], axis=1)


def step_kernel(rate_ref, index_ref, labels_ref, order_ref, adjoint_ref, order_halo_ref, adjoint_halo_ref,
                own_ref, other_ref, order_next_ref, adjoint_order_ref):
    p = pl.program_id(0)
    rate = 0.1 * rate_ref[p]
    index = index_ref[p]
    rows = order_ref.shape[1]
    depth = order_ref.shape[2]
    width = order_ref.shape[3]
    level = lax.broadcasted_iota(jnp.int32, (depth, width), 0)
    top = level == depth - 1
    bottom = level == 0

    def laplace(centre, before, after):
        beside = before + after
        beside = beside + pltpu.roll(centre, 1, 1) + pltpu.roll(centre, width - 1, 1)
        upper = jnp.where(top, centre, pltpu.roll(centre, depth - 1, 0))
        lower = jnp.where(bottom, centre, pltpu.roll(centre, 1, 0))
        return beside + upper + lower - 6.0 * centre

    def order_row(j):
        if j < 0:
            return order_halo_ref[0, 0]
        if j >= rows:
            return order_halo_ref[0, 1]
        return order_ref[0, j]

    def weight_row(j):
        if j < 0:
            return rate * adjoint_halo_ref[0, 0]
        if j >= rows:
            return rate * adjoint_halo_ref[0, 1]
        return rate * adjoint_ref[0, j]

    for j in range(rows):
        o = order_row(j)
        adj = adjoint_ref[0, j]
        w = rate * adj
        squares = own_ref[0, j] + other_ref[0, j]
        coupled = own_ref[1, j] + other_ref[1, j]
        foreign = (labels_ref[j : j + 1, :] != index).astype(jnp.float32)
        sign = -1.0 + 2.0 * foreign
        potential = sign * o - 2.0 * (o * o * o) + 3.0 * o * squares - 0.5 * laplace(o, order_row(j - 1), order_row(j + 1))
        order_next_ref[0, j] = o - rate * potential
        local_part = (sign - 6.0 * o * o + 3.0 * squares) * w
        adjoint_order_ref[0, j] = adj - (local_part + 6.0 * o * coupled - 0.5 * laplace(w, weight_row(j - 1), weight_row(j + 1)))


def local(order_field, adjoint_next, mobility, labels):
    count, rows, depth, width = order_field.shape
    first = lax.axis_index("op") * count
    indices = first + jnp.arange(count, dtype=jnp.int32)
    rates = mobility[:, None, None, None]
    weighted = 0.1 * rates * adjoint_next
    own = jnp.stack([jnp.sum(order_field * order_field, axis=0), jnp.sum(order_field * weighted, axis=0)])
    parts = lax.axis_size("op")
    other = lax.ppermute(own, "op", [(i, (i + 1) % parts) for i in range(parts)])
    order_halo = neighbour_rows(order_field, "space")
    adjoint_halo = neighbour_rows(adjoint_next, "space")
    block = pl.BlockSpec((1, rows, depth, width), lambda p, *_: (p, 0, 0, 0))
    halo = pl.BlockSpec((1, 2, depth, width), lambda p, *_: (p, 0, 0, 0))
    sums = pl.BlockSpec((2, rows, depth, width), lambda p, *_: (0, 0, 0, 0))
    grid_spec = pltpu.PrefetchScalarGridSpec(
        num_scalar_prefetch=2,
        grid=(count,),
        in_specs=[
            pl.BlockSpec((rows, width), lambda p, *_: (0, 0)),
            block,
            block,
            halo,
            halo,
            sums,
            sums,
        ],
        out_specs=[block, block],
    )
    return pl.pallas_call(
        step_kernel,
        grid_spec=grid_spec,
        out_shape=[jax.ShapeDtypeStruct(order_field.shape, jnp.float32)] * 2,
    )(mobility, indices, labels, order_field, adjoint_next, order_halo, adjoint_halo, own, other)


def solution(mesh):
    placed = (P("op", "space", None, None), P("op", "space", None, None), P("op"), P("space", None))
    return jax.shard_map(
        local,
        mesh=mesh,
        in_specs=placed,
        out_specs=(P("op", "space", None, None), P("op", "space", None, None)),
        check_vma=False,
    )
```

```python
import jax
import jax.numpy as jnp
from jax import lax
from jax.experimental import pallas as pl
from jax.experimental.pallas import tpu as pltpu
from jax.sharding import PartitionSpec as P


def shift_along(cells, axis, step):
    count = lax.axis_size(axis)
    return lax.ppermute(cells, axis, [(i, (i + step) % count) for i in range(count)])


def step_kernel(rate_ref, index_ref, labels_ref, order_ref, adjoint_ref, below_ref, above_ref,
                own_ref, other_ref, order_next_ref, adjoint_order_ref):
    p = pl.program_id(0)
    rate = 0.1 * rate_ref[p]
    index = index_ref[p]
    rows = order_ref.shape[1]
    depth = order_ref.shape[2]
    width = order_ref.shape[3]
    level = lax.broadcasted_iota(jnp.int32, (depth, width), 0)
    top = level == depth - 1
    bottom = level == 0

    def laplace(centre, before, after):
        beside = before + after
        beside = beside + pltpu.roll(centre, 1, 1) + pltpu.roll(centre, width - 1, 1)
        upper = jnp.where(top, centre, pltpu.roll(centre, depth - 1, 0))
        lower = jnp.where(bottom, centre, pltpu.roll(centre, 1, 0))
        return beside + upper + lower - 6.0 * centre

    def load(j):
        if j < 0:
            return below_ref[0, 0, 0], rate * below_ref[1, 0, 0]
        if j >= rows:
            return above_ref[0, 0, 0], rate * above_ref[1, 0, 0]
        return order_ref[0, j], rate * adjoint_ref[0, j]

    prev = load(-1)
    cur = load(0)
    for j in range(rows):
        nxt = load(j + 1)
        o, w = cur
        adj = adjoint_ref[0, j]
        squares = own_ref[0, j] + other_ref[0, j]
        coupled = own_ref[1, j] + other_ref[1, j]
        sign = jnp.where(labels_ref[j : j + 1, :] != index, 1.0, -1.0)
        potential = sign * o - 2.0 * (o * o * o) + 3.0 * o * squares - 0.5 * laplace(o, prev[0], nxt[0])
        order_next_ref[0, j] = o - rate * potential
        local_part = (sign - 6.0 * o * o + 3.0 * squares) * w
        adjoint_order_ref[0, j] = adj - (local_part + 6.0 * o * coupled - 0.5 * laplace(w, prev[1], nxt[1]))
        prev, cur = cur, nxt


def local(order_field, adjoint_next, mobility, labels):
    count, rows, depth, width = order_field.shape
    first = lax.axis_index("op") * count
    indices = first + jnp.arange(count, dtype=jnp.int32)
    rates = mobility[:, None, None, None]
    weighted = 0.1 * rates * adjoint_next
    own = jnp.stack([jnp.sum(order_field * order_field, axis=0), jnp.sum(order_field * weighted, axis=0)])
    other = shift_along(own, "op", 1)
    pair = jnp.stack([order_field, adjoint_next])
    edges = jnp.concatenate([pair[:, :, :1], pair[:, :, -1:]], axis=2)
    edges, own = lax.optimization_barrier((edges, own))
    below = shift_along(edges[:, :, 1:], "space", 1)
    above = shift_along(edges[:, :, :1], "space", -1)
    block = pl.BlockSpec((1, rows, depth, width), lambda p, *_: (p, 0, 0, 0))
    halo = pl.BlockSpec((2, 1, 1, depth, width), lambda p, *_: (0, p, 0, 0, 0))
    sums = pl.BlockSpec((2, rows, depth, width), lambda p, *_: (0, 0, 0, 0))
    grid_spec = pltpu.PrefetchScalarGridSpec(
        num_scalar_prefetch=2,
        grid=(count,),
        in_specs=[pl.BlockSpec((rows, width), lambda p, *_: (0, 0)), block, block, halo, halo, sums, sums],
        out_specs=[block, block],
    )
    return pl.pallas_call(
        step_kernel,
        grid_spec=grid_spec,
        out_shape=[jax.ShapeDtypeStruct(order_field.shape, jnp.float32)] * 2,
    )(mobility, indices, labels, order_field, adjoint_next, below, above, own, other)


def solution(mesh):
    placed = (P("op", "space", None, None), P("op", "space", None, None), P("op"), P("space", None))
    return jax.shard_map(
        local,
        mesh=mesh,
        in_specs=placed,
        out_specs=(P("op", "space", None, None), P("op", "space", None, None)),
        check_vma=False,
    )
```

```python
import jax
import jax.numpy as jnp
from jax import lax
from jax.experimental import pallas as pl
from jax.experimental.pallas import tpu as pltpu
from jax.sharding import PartitionSpec as P


def shift_along(cells, axis, step):
    count = lax.axis_size(axis)
    return lax.ppermute(cells, axis, [(i, (i + step) % count) for i in range(count)])


def stencil(depth, width):
    level = lax.broadcasted_iota(jnp.int32, (depth, width), 0)
    top = level == depth - 1
    bottom = level == 0

    def laplace(centre, before, after):
        beside = before + after
        beside = beside + pltpu.roll(centre, 1, 1) + pltpu.roll(centre, width - 1, 1)
        upper = jnp.where(top, centre, pltpu.roll(centre, depth - 1, 0))
        lower = jnp.where(bottom, centre, pltpu.roll(centre, 1, 0))
        return beside + upper + lower - 6.0 * centre

    return laplace


def inner_kernel(rate_ref, index_ref, labels_ref, order_ref, adjoint_ref, inner_order_ref, inner_adjoint_ref):
    p = pl.program_id(0)
    rate = 0.1 * rate_ref[p]
    index = index_ref[p]
    _, rows, depth, width = order_ref.shape
    laplace = stencil(depth, width)

    def load(j):
        return order_ref[0, j], rate * adjoint_ref[0, j]

    prev = load(0)
    cur = load(1)
    for j in range(1, rows - 1):
        nxt = load(j + 1)
        o, w = cur
        sign = jnp.where(labels_ref[j : j + 1, :] != index, 1.0, -1.0)
        inner_order_ref[0, j - 1] = sign * o - 2.0 * (o * o * o) - 0.5 * laplace(o, prev[0], nxt[0])
        inner_adjoint_ref[0, j - 1] = (sign - 6.0 * o * o) * w - 0.5 * laplace(w, prev[1], nxt[1])
        prev, cur = cur, nxt


def step_kernel(rate_ref, index_ref, labels_ref, order_ref, adjoint_ref, below_ref, above_ref,
                own_ref, other_ref, inner_order_ref, inner_adjoint_ref, order_next_ref, adjoint_order_ref):
    p = pl.program_id(0)
    rate = 0.1 * rate_ref[p]
    index = index_ref[p]
    _, rows, depth, width = order_ref.shape
    laplace = stencil(depth, width)

    def load(j):
        if j < 0:
            return below_ref[0, 0, 0], rate * below_ref[1, 0, 0]
        if j >= rows:
            return above_ref[0, 0, 0], rate * above_ref[1, 0, 0]
        return order_ref[0, j], rate * adjoint_ref[0, j]

    for j in range(rows):
        o, w = load(j)
        adj = adjoint_ref[0, j]
        squares = own_ref[0, j] + other_ref[0, j]
        coupled = own_ref[1, j] + other_ref[1, j]
        if 0 < j < rows - 1:
            order_next_ref[0, j] = o - rate * (inner_order_ref[0, j - 1] + 3.0 * o * squares)
            adjoint_order_ref[0, j] = adj - ((inner_adjoint_ref[0, j - 1] + 3.0 * squares * w) + 6.0 * o * coupled)
            continue
        prev = load(j - 1)
        nxt = load(j + 1)
        sign = jnp.where(labels_ref[j : j + 1, :] != index, 1.0, -1.0)
        potential = sign * o - 2.0 * (o * o * o) + 3.0 * o * squares - 0.5 * laplace(o, prev[0], nxt[0])
        order_next_ref[0, j] = o - rate * potential
        local_part = (sign - 6.0 * o * o + 3.0 * squares) * w
        adjoint_order_ref[0, j] = adj - (local_part + 6.0 * o * coupled - 0.5 * laplace(w, prev[1], nxt[1]))


def local(order_field, adjoint_next, mobility, labels):
    count, rows, depth, width = order_field.shape
    first = lax.axis_index("op") * count
    indices = first + jnp.arange(count, dtype=jnp.int32)
    rates = mobility[:, None, None, None]
    weighted = 0.1 * rates * adjoint_next
    own = jnp.stack([jnp.sum(order_field * order_field, axis=0), jnp.sum(order_field * weighted, axis=0)])
    other = shift_along(own, "op", 1)
    pair = jnp.stack([order_field, adjoint_next])
    edges = jnp.concatenate([pair[:, :, :1], pair[:, :, -1:]], axis=2)
    edges, own, order_late, adjoint_late = lax.optimization_barrier((edges, own, order_field, adjoint_next))
    below = shift_along(edges[:, :, 1:], "space", 1)
    above = shift_along(edges[:, :, :1], "space", -1)
    scalars = pltpu.PrefetchScalarGridSpec
    block = pl.BlockSpec((1, rows, depth, width), lambda p, *_: (p, 0, 0, 0))
    inner = pl.BlockSpec((1, rows - 2, depth, width), lambda p, *_: (p, 0, 0, 0))
    plane = pl.BlockSpec((rows, width), lambda p, *_: (0, 0))
    inner_order, inner_adjoint = pl.pallas_call(
        inner_kernel,
        grid_spec=scalars(num_scalar_prefetch=2, grid=(count,), in_specs=[plane, block, block], out_specs=[inner, inner]),
        out_shape=[jax.ShapeDtypeStruct((count, rows - 2, depth, width), jnp.float32)] * 2,
    )(mobility, indices, labels, order_late, adjoint_late)
    halo = pl.BlockSpec((2, 1, 1, depth, width), lambda p, *_: (0, p, 0, 0, 0))
    sums = pl.BlockSpec((2, rows, depth, width), lambda p, *_: (0, 0, 0, 0))
    return pl.pallas_call(
        step_kernel,
        grid_spec=scalars(
            num_scalar_prefetch=2,
            grid=(count,),
            in_specs=[plane, block, block, halo, halo, sums, sums, inner, inner],
            out_specs=[block, block],
        ),
        out_shape=[jax.ShapeDtypeStruct(order_field.shape, jnp.float32)] * 2,
    )(mobility, indices, labels, order_field, adjoint_next, below, above, own, other, inner_order, inner_adjoint)


def solution(mesh):
    placed = (P("op", "space", None, None), P("op", "space", None, None), P("op"), P("space", None))
    return jax.shard_map(
        local,
        mesh=mesh,
        in_specs=placed,
        out_specs=(P("op", "space", None, None), P("op", "space", None, None)),
        check_vma=False,
    )
```

```python
import jax
import jax.numpy as jnp
from jax import lax
from jax.experimental import pallas as pl
from jax.experimental.pallas import tpu as pltpu
from jax.sharding import PartitionSpec as P


def shift_along(cells, axis, step):
    count = lax.axis_size(axis)
    return lax.ppermute(cells, axis, [(i, (i + step) % count) for i in range(count)])


def stencil(depth, width):
    level = lax.broadcasted_iota(jnp.int32, (depth, width), 0)
    top = level == depth - 1
    bottom = level == 0

    def laplace(centre, beside):
        beside = beside + pltpu.roll(centre, 1, 1) + pltpu.roll(centre, width - 1, 1)
        upper = jnp.where(top, centre, pltpu.roll(centre, depth - 1, 0))
        lower = jnp.where(bottom, centre, pltpu.roll(centre, 1, 0))
        return beside + upper + lower - 6.0 * centre

    return laplace


def inner_kernel(rate_ref, index_ref, labels_ref, order_ref, adjoint_ref, inner_order_ref, inner_adjoint_ref):
    p = pl.program_id(0)
    rate = 0.1 * rate_ref[p]
    index = index_ref[p]
    _, rows, depth, width = order_ref.shape
    laplace = stencil(depth, width)

    def load(j):
        return order_ref[0, j], rate * adjoint_ref[0, j]

    prev = None
    cur = load(0)
    for j in range(rows):
        nxt = load(j + 1) if j + 1 < rows else None
        o, w = cur
        if prev is None:
            beside = nxt
        elif nxt is None:
            beside = prev
        else:
            beside = (prev[0] + nxt[0], prev[1] + nxt[1])
        sign = jnp.where(labels_ref[j : j + 1, :] != index, 1.0, -1.0)
        inner_order_ref[0, j] = sign * o - 2.0 * (o * o * o) - 0.5 * laplace(o, beside[0])
        inner_adjoint_ref[0, j] = (sign - 6.0 * o * o) * w - 0.5 * laplace(w, beside[1])
        prev, cur = cur, nxt


def final_kernel(rate_ref, order_ref, adjoint_ref, sums_ref, inner_order_ref, inner_adjoint_ref,
                 order_next_ref, adjoint_order_ref):
    p = pl.program_id(0)
    rate = 0.1 * rate_ref[p]
    rows = order_ref.shape[1]
    for j in range(rows):
        o = order_ref[0, j]
        adj = adjoint_ref[0, j]
        w = rate * adj
        squares = sums_ref[0, j]
        order_next_ref[0, j] = o - rate * (inner_order_ref[0, j] + o * squares)
        adjoint_order_ref[0, j] = adj - ((inner_adjoint_ref[0, j] + w * squares) + o * sums_ref[1, j])


def edge_kernel(rate_ref, below_ref, above_ref, order_next_in, adjoint_order_in, order_next_ref, adjoint_order_ref):
    side = pl.program_id(0)
    count = order_next_in.shape[0]
    for p in range(count):
        rate = 0.1 * rate_ref[p]
        order_row = jnp.where(side == 0, below_ref[0, p, 0], above_ref[0, p, 0])
        adjoint_row = jnp.where(side == 0, below_ref[1, p, 0], above_ref[1, p, 0])
        order_next_ref[p, 0] = order_next_in[p, 0] + (0.5 * rate) * order_row
        adjoint_order_ref[p, 0] = adjoint_order_in[p, 0] + 0.5 * (rate * adjoint_row)


def local(order_field, adjoint_next, mobility, labels):
    count, rows, depth, width = order_field.shape
    first = lax.axis_index("op") * count
    indices = first + jnp.arange(count, dtype=jnp.int32)
    rates = mobility[:, None, None, None]
    weighted = 0.1 * rates * adjoint_next
    own = jnp.stack([jnp.sum(order_field * order_field, axis=0), jnp.sum(order_field * weighted, axis=0)])
    other = shift_along(own, "op", 1)
    pair = jnp.stack([order_field, adjoint_next])
    edges = jnp.concatenate([pair[:, :, :1], pair[:, :, -1:]], axis=2)
    edges, own, order_late, adjoint_late = lax.optimization_barrier((edges, own, order_field, adjoint_next))
    below = shift_along(edges[:, :, 1:], "space", 1)
    above = shift_along(edges[:, :, :1], "space", -1)
    scalars = pltpu.PrefetchScalarGridSpec
    block = pl.BlockSpec((1, rows, depth, width), lambda p, *_: (p, 0, 0, 0))
    plane = pl.BlockSpec((rows, width), lambda p, *_: (0, 0))
    inner_order, inner_adjoint = pl.pallas_call(
        inner_kernel,
        grid_spec=scalars(num_scalar_prefetch=2, grid=(count,), in_specs=[plane, block, block], out_specs=[block, block]),
        out_shape=[jax.ShapeDtypeStruct(order_field.shape, jnp.float32)] * 2,
    )(mobility, indices, labels, order_late, adjoint_late)
    total = own + other
    sums = jnp.stack([3.0 * total[0], 6.0 * total[1]])
    whole = pl.BlockSpec((2, rows, depth, width), lambda p, *_: (0, 0, 0, 0))
    order_next, adjoint_order = pl.pallas_call(
        final_kernel,
        grid_spec=scalars(num_scalar_prefetch=1, grid=(count,), in_specs=[block, block, whole, block, block], out_specs=[block, block]),
        out_shape=[jax.ShapeDtypeStruct(order_field.shape, jnp.float32)] * 2,
    )(mobility, order_field, adjoint_next, sums, inner_order, inner_adjoint)
    halo = pl.BlockSpec((2, count, 1, depth, width), lambda s, *_: (0, 0, 0, 0, 0))
    row = pl.BlockSpec((count, 1, depth, width), lambda s, *_: (0, s * (rows - 1), 0, 0))
    return pl.pallas_call(
        edge_kernel,
        grid_spec=scalars(num_scalar_prefetch=1, grid=(2,), in_specs=[halo, halo, row, row], out_specs=[row, row]),
        out_shape=[jax.ShapeDtypeStruct(order_field.shape, jnp.float32)] * 2,
        input_output_aliases={3: 0, 4: 1},
    )(mobility, below, above, order_next, adjoint_order)


def solution(mesh):
    placed = (P("op", "space", None, None), P("op", "space", None, None), P("op"), P("space", None))
    return jax.shard_map(
        local,
        mesh=mesh,
        in_specs=placed,
        out_specs=(P("op", "space", None, None), P("op", "space", None, None)),
        check_vma=False,
    )
```

```python
import jax
import jax.numpy as jnp
from jax import lax
from jax.experimental import pallas as pl
from jax.experimental.pallas import tpu as pltpu
from jax.sharding import PartitionSpec as P


def shift_along(cells, axis, step):
    count = lax.axis_size(axis)
    return lax.ppermute(cells, axis, [(i, (i + step) % count) for i in range(count)])


def stencil(depth, width):
    level = lax.broadcasted_iota(jnp.int32, (depth, width), 0)
    top = level == depth - 1
    bottom = level == 0

    def laplace(centre, beside):
        beside = beside + pltpu.roll(centre, 1, 1) + pltpu.roll(centre, width - 1, 1)
        upper = jnp.where(top, centre, pltpu.roll(centre, depth - 1, 0))
        lower = jnp.where(bottom, centre, pltpu.roll(centre, 1, 0))
        return beside + upper + lower - 6.0 * centre

    return laplace


def inner_kernel(rate_ref, index_ref, labels_ref, order_ref, adjoint_ref, inner_order_ref, inner_adjoint_ref):
    p = pl.program_id(0)
    rate = 0.1 * rate_ref[p]
    index = index_ref[p]
    _, rows, depth, width = order_ref.shape
    laplace = stencil(depth, width)

    def load(j):
        return order_ref[0, j], rate * adjoint_ref[0, j]

    prev = None
    cur = load(0)
    for j in range(rows):
        nxt = load(j + 1) if j + 1 < rows else None
        o, w = cur
        if prev is None:
            beside = nxt
        elif nxt is None:
            beside = prev
        else:
            beside = (prev[0] + nxt[0], prev[1] + nxt[1])
        sign = jnp.where(labels_ref[j : j + 1, :] != index, 1.0, -1.0)
        inner_order_ref[0, j] = sign * o - 2.0 * (o * o * o) - 0.5 * laplace(o, beside[0])
        inner_adjoint_ref[0, j] = (sign - 6.0 * o * o) * w - 0.5 * laplace(w, beside[1])
        prev, cur = cur, nxt


def final_kernel(rate_ref, order_ref, adjoint_ref, sums_ref, inner_order_ref, inner_adjoint_ref,
                 order_next_ref, adjoint_order_ref):
    p = pl.program_id(0)
    rate = 0.1 * rate_ref[p]
    rows = order_ref.shape[1]
    for j in range(rows):
        o = order_ref[0, j]
        adj = adjoint_ref[0, j]
        w = rate * adj
        squares = sums_ref[0, j]
        order_next_ref[0, j] = o - rate * (inner_order_ref[0, j] + o * squares)
        adjoint_order_ref[0, j] = adj - ((inner_adjoint_ref[0, j] + w * squares) + o * sums_ref[1, j])


def edge_kernel(rate_ref, below_ref, above_ref, order_next_in, adjoint_order_in, order_next_ref, adjoint_order_ref):
    side = pl.program_id(0)
    count = order_next_in.shape[0]
    for p in range(count):
        rate = 0.1 * rate_ref[p]
        order_row = jnp.where(side == 0, below_ref[0, p, 0], above_ref[0, p, 0])
        adjoint_row = jnp.where(side == 0, below_ref[1, p, 0], above_ref[1, p, 0])
        order_next_ref[p, 0] = order_next_in[p, 0] + (0.5 * rate) * order_row
        adjoint_order_ref[p, 0] = adjoint_order_in[p, 0] + 0.5 * (rate * adjoint_row)


def local(order_field, adjoint_next, mobility, labels):
    count, rows, depth, width = order_field.shape
    first = lax.axis_index("op") * count
    indices = first + jnp.arange(count, dtype=jnp.int32)
    rates = mobility[:, None, None, None]
    weighted = 0.1 * rates * adjoint_next
    own = jnp.stack([jnp.sum(order_field * order_field, axis=0), jnp.sum(order_field * weighted, axis=0)])
    other = shift_along(own, "op", 1)
    pair = jnp.stack([order_field, adjoint_next])
    edges = jnp.concatenate([pair[:, :, :1], pair[:, :, -1:]], axis=2)
    edges, own, order_late, adjoint_late = lax.optimization_barrier((edges, own, order_field, adjoint_next))
    below = shift_along(edges[:, :, 1:], "space", 1)
    above = shift_along(edges[:, :, :1], "space", -1)
    scalars = pltpu.PrefetchScalarGridSpec
    block = pl.BlockSpec((1, rows, depth, width), lambda p, *_: (p, 0, 0, 0))
    plane = pl.BlockSpec((rows, width), lambda p, *_: (0, 0))
    inner_order, inner_adjoint = pl.pallas_call(
        inner_kernel,
        grid_spec=scalars(num_scalar_prefetch=2, grid=(count,), in_specs=[plane, block, block], out_specs=[block, block]),
        out_shape=[jax.ShapeDtypeStruct(order_field.shape, jnp.float32)] * 2,
    )(mobility, indices, labels, order_late, adjoint_late)
    total = own + other
    sums = jnp.stack([3.0 * total[0], 6.0 * total[1]])
    whole = pl.BlockSpec((2, rows, depth, width), lambda p, *_: (0, 0, 0, 0))
    order_next, adjoint_order = pl.pallas_call(
        final_kernel,
        grid_spec=scalars(num_scalar_prefetch=1, grid=(count,), in_specs=[block, block, whole, block, block], out_specs=[block, block]),
        out_shape=[jax.ShapeDtypeStruct(order_field.shape, jnp.float32)] * 2,
    )(mobility, order_field, adjoint_next, sums, inner_order, inner_adjoint)
    on_chip = pl.BlockSpec(memory_space=pltpu.VMEM)
    row = pl.BlockSpec((count, 1, depth, width), lambda s, *_: (0, s * (rows - 1), 0, 0))
    return pl.pallas_call(
        edge_kernel,
        grid_spec=scalars(num_scalar_prefetch=1, grid=(2,), in_specs=[on_chip, on_chip, row, row], out_specs=[row, row]),
        out_shape=[jax.ShapeDtypeStruct(order_field.shape, jnp.float32)] * 2,
        input_output_aliases={3: 0, 4: 1},
    )(mobility, *[pltpu.with_memory_space_constraint(x, pltpu.VMEM) for x in (below, above)], order_next, adjoint_order)


def solution(mesh):
    placed = (P("op", "space", None, None), P("op", "space", None, None), P("op"), P("space", None))
    return jax.shard_map(
        local,
        mesh=mesh,
        in_specs=placed,
        out_specs=(P("op", "space", None, None), P("op", "space", None, None)),
        check_vma=False,
    )
```

```python
import jax
import jax.numpy as jnp
from jax import lax
from jax.experimental import pallas as pl
from jax.experimental.pallas import tpu as pltpu
from jax.sharding import PartitionSpec as P


def shift_along(cells, axis, step):
    count = lax.axis_size(axis)
    return lax.ppermute(cells, axis, [(i, (i + step) % count) for i in range(count)])


def stencil(depth, width):
    level = lax.broadcasted_iota(jnp.int32, (depth, width), 0)
    top = level == depth - 1
    bottom = level == 0

    def laplace(centre, beside):
        beside = beside + pltpu.roll(centre, 1, 1) + pltpu.roll(centre, width - 1, 1)
        upper = jnp.where(top, centre, pltpu.roll(centre, depth - 1, 0))
        lower = jnp.where(bottom, centre, pltpu.roll(centre, 1, 0))
        return beside + upper + lower - 6.0 * centre

    return laplace


def inner_kernel(rate_ref, index_ref, labels_ref, order_ref, adjoint_ref, inner_order_ref, inner_adjoint_ref):
    p = pl.program_id(0)
    rate = 0.1 * rate_ref[p]
    index = index_ref[p]
    _, rows, depth, width = order_ref.shape
    laplace = stencil(depth, width)

    def load(j):
        return order_ref[0, j], rate * adjoint_ref[0, j]

    prev = None
    cur = load(0)
    for j in range(rows):
        nxt = load(j + 1) if j + 1 < rows else None
        o, w = cur
        if prev is None:
            beside = nxt
        elif nxt is None:
            beside = prev
        else:
            beside = (prev[0] + nxt[0], prev[1] + nxt[1])
        sign = jnp.where(labels_ref[j : j + 1, :] != index, 1.0, -1.0)
        inner_order_ref[0, j] = sign * o - 2.0 * (o * o * o) - 0.5 * laplace(o, beside[0])
        inner_adjoint_ref[0, j] = (sign - 6.0 * o * o) * w - 0.5 * laplace(w, beside[1])
        prev, cur = cur, nxt


def sums_kernel(rate_ref, order_ref, adjoint_ref, own_ref):
    count, rows = order_ref.shape[:2]
    for j in range(rows):
        squares = None
        coupled = None
        for p in range(count):
            o = order_ref[p, j]
            w = (0.1 * rate_ref[p]) * adjoint_ref[p, j]
            squares = o * o if squares is None else squares + o * o
            coupled = o * w if coupled is None else coupled + o * w
        own_ref[0, j] = squares
        own_ref[1, j] = coupled


def final_kernel(rate_ref, order_ref, adjoint_ref, own_ref, other_ref, inner_order_ref, inner_adjoint_ref,
                 order_next_ref, adjoint_order_ref):
    p = pl.program_id(0)
    rate = 0.1 * rate_ref[p]
    rows = order_ref.shape[1]
    for j in range(rows):
        o = order_ref[0, j]
        adj = adjoint_ref[0, j]
        w = rate * adj
        squares = 3.0 * (own_ref[0, j] + other_ref[0, j])
        coupled = 6.0 * (own_ref[1, j] + other_ref[1, j])
        order_next_ref[0, j] = o - rate * (inner_order_ref[0, j] + o * squares)
        adjoint_order_ref[0, j] = adj - ((inner_adjoint_ref[0, j] + w * squares) + o * coupled)


def edge_kernel(rate_ref, below_ref, above_ref, order_next_in, adjoint_order_in, order_next_ref, adjoint_order_ref):
    side = pl.program_id(0)
    count = order_next_in.shape[0]
    for p in range(count):
        rate = 0.1 * rate_ref[p]
        order_row = jnp.where(side == 0, below_ref[0, p, 0], above_ref[0, p, 0])
        adjoint_row = jnp.where(side == 0, below_ref[1, p, 0], above_ref[1, p, 0])
        order_next_ref[p, 0] = order_next_in[p, 0] + (0.5 * rate) * order_row
        adjoint_order_ref[p, 0] = adjoint_order_in[p, 0] + 0.5 * (rate * adjoint_row)


def local(order_field, adjoint_next, mobility, labels):
    count, rows, depth, width = order_field.shape
    first = lax.axis_index("op") * count
    indices = first + jnp.arange(count, dtype=jnp.int32)
    step = 2
    chunk = pl.BlockSpec((count, step, depth, width), lambda r, *_: (0, r, 0, 0))
    own = pl.pallas_call(
        sums_kernel,
        grid_spec=pltpu.PrefetchScalarGridSpec(
            num_scalar_prefetch=1,
            grid=(rows // step,),
            in_specs=[chunk, chunk],
            out_specs=pl.BlockSpec((2, step, depth, width), lambda r, *_: (0, r, 0, 0)),
        ),
        out_shape=jax.ShapeDtypeStruct((2, rows, depth, width), jnp.float32),
    )(mobility, order_field, adjoint_next)
    other = shift_along(own, "op", 1)
    pair = jnp.stack([order_field, adjoint_next])
    edges = jnp.concatenate([pair[:, :, :1], pair[:, :, -1:]], axis=2)
    edges, own, order_late, adjoint_late = lax.optimization_barrier((edges, own, order_field, adjoint_next))
    below = shift_along(edges[:, :, 1:], "space", 1)
    above = shift_along(edges[:, :, :1], "space", -1)
    scalars = pltpu.PrefetchScalarGridSpec
    block = pl.BlockSpec((1, rows, depth, width), lambda p, *_: (p, 0, 0, 0))
    plane = pl.BlockSpec((rows, width), lambda p, *_: (0, 0))
    inner_order, inner_adjoint = pl.pallas_call(
        inner_kernel,
        grid_spec=scalars(num_scalar_prefetch=2, grid=(count,), in_specs=[plane, block, block], out_specs=[block, block]),
        out_shape=[jax.ShapeDtypeStruct(order_field.shape, jnp.float32)] * 2,
    )(mobility, indices, labels, order_late, adjoint_late)
    on_chip = pl.BlockSpec(memory_space=pltpu.VMEM)
    order_next, adjoint_order = pl.pallas_call(
        final_kernel,
        grid_spec=scalars(num_scalar_prefetch=1, grid=(count,), in_specs=[block, block, on_chip, on_chip, block, block], out_specs=[block, block]),
        out_shape=[jax.ShapeDtypeStruct(order_field.shape, jnp.float32)] * 2,
    )(mobility, order_field, adjoint_next, *[pltpu.with_memory_space_constraint(x, pltpu.VMEM) for x in (own, other)],
      inner_order, inner_adjoint)
    row = pl.BlockSpec((count, 1, depth, width), lambda s, *_: (0, s * (rows - 1), 0, 0))
    return pl.pallas_call(
        edge_kernel,
        grid_spec=scalars(num_scalar_prefetch=1, grid=(2,), in_specs=[on_chip, on_chip, row, row], out_specs=[row, row]),
        out_shape=[jax.ShapeDtypeStruct(order_field.shape, jnp.float32)] * 2,
        input_output_aliases={3: 0, 4: 1},
    )(mobility, *[pltpu.with_memory_space_constraint(x, pltpu.VMEM) for x in (below, above)], order_next, adjoint_order)


def solution(mesh):
    placed = (P("op", "space", None, None), P("op", "space", None, None), P("op"), P("space", None))
    return jax.shard_map(
        local,
        mesh=mesh,
        in_specs=placed,
        out_specs=(P("op", "space", None, None), P("op", "space", None, None)),
        check_vma=False,
    )
```

```python
import jax
import jax.numpy as jnp
from jax import lax
from jax.experimental import pallas as pl
from jax.experimental.pallas import tpu as pltpu
from jax.sharding import PartitionSpec as P


def shift_along(cells, axis, step):
    count = lax.axis_size(axis)
    return lax.ppermute(cells, axis, [(i, (i + step) % count) for i in range(count)])


def stencil(depth, width):
    level = lax.broadcasted_iota(jnp.int32, (depth, width), 0)
    top = level == depth - 1
    bottom = level == 0

    def laplace(centre, beside):
        beside = beside + pltpu.roll(centre, 1, 1) + pltpu.roll(centre, width - 1, 1)
        upper = jnp.where(top, centre, pltpu.roll(centre, depth - 1, 0))
        lower = jnp.where(bottom, centre, pltpu.roll(centre, 1, 0))
        return beside + upper + lower - 6.0 * centre

    return laplace


def inner_kernel(rate_ref, index_ref, labels_ref, order_ref, adjoint_ref, inner_order_ref, inner_adjoint_ref):
    p = pl.program_id(0)
    rate = 0.1 * rate_ref[p]
    index = index_ref[p]
    _, rows, depth, width = order_ref.shape
    laplace = stencil(depth, width)

    def load(j):
        return order_ref[0, j], rate * adjoint_ref[0, j]

    prev = None
    cur = load(0)
    for j in range(rows):
        nxt = load(j + 1) if j + 1 < rows else None
        o, w = cur
        if prev is None:
            beside = nxt
        elif nxt is None:
            beside = prev
        else:
            beside = (prev[0] + nxt[0], prev[1] + nxt[1])
        sign = jnp.where(labels_ref[j : j + 1, :] != index, 1.0, -1.0)
        inner_order_ref[0, j] = sign * o - 2.0 * (o * o * o) - 0.5 * laplace(o, beside[0])
        inner_adjoint_ref[0, j] = (sign - 6.0 * o * o) * w - 0.5 * laplace(w, beside[1])
        prev, cur = cur, nxt


def final_kernel(rate_ref, order_ref, adjoint_ref, own_ref, other_ref, inner_order_ref, inner_adjoint_ref,
                 order_next_ref, adjoint_order_ref):
    p = pl.program_id(0)
    rate = 0.1 * rate_ref[p]
    rows = order_ref.shape[1]
    for j in range(rows):
        o = order_ref[0, j]
        adj = adjoint_ref[0, j]
        w = rate * adj
        squares = 3.0 * (own_ref[0, j] + other_ref[0, j])
        coupled = 6.0 * (own_ref[1, j] + other_ref[1, j])
        order_next_ref[0, j] = o - rate * (inner_order_ref[0, j] + o * squares)
        adjoint_order_ref[0, j] = adj - ((inner_adjoint_ref[0, j] + w * squares) + o * coupled)


def edge_kernel(rate_ref, below_ref, above_ref, order_next_in, adjoint_order_in, order_next_ref, adjoint_order_ref):
    side = pl.program_id(0)
    count = order_next_in.shape[0]
    for p in range(count):
        rate = 0.1 * rate_ref[p]
        order_row = jnp.where(side == 0, below_ref[0, p, 0], above_ref[0, p, 0])
        adjoint_row = jnp.where(side == 0, below_ref[1, p, 0], above_ref[1, p, 0])
        order_next_ref[p, 0] = order_next_in[p, 0] + (0.5 * rate) * order_row
        adjoint_order_ref[p, 0] = adjoint_order_in[p, 0] + 0.5 * (rate * adjoint_row)


def local(order_field, adjoint_next, mobility, labels):
    count, rows, depth, width = order_field.shape
    first = lax.axis_index("op") * count
    indices = first + jnp.arange(count, dtype=jnp.int32)
    rates = mobility[:, None, None, None]
    weighted = 0.1 * rates * adjoint_next
    own = jnp.stack([jnp.sum(order_field * order_field, axis=0), jnp.sum(order_field * weighted, axis=0)])
    other = shift_along(own, "op", 1)
    pair = jnp.stack([order_field, adjoint_next])
    edges = jnp.concatenate([pair[:, :, :1], pair[:, :, -1:]], axis=2)
    edges, own, order_late, adjoint_late = lax.optimization_barrier((edges, own, order_field, adjoint_next))
    below = shift_along(edges[:, :, 1:], "space", 1)
    above = shift_along(edges[:, :, :1], "space", -1)
    scalars = pltpu.PrefetchScalarGridSpec
    block = pl.BlockSpec((1, rows, depth, width), lambda p, *_: (p, 0, 0, 0))
    plane = pl.BlockSpec((rows, width), lambda p, *_: (0, 0))
    inner_order, inner_adjoint = pl.pallas_call(
        inner_kernel,
        grid_spec=scalars(num_scalar_prefetch=2, grid=(count,), in_specs=[plane, block, block], out_specs=[block, block]),
        out_shape=[jax.ShapeDtypeStruct(order_field.shape, jnp.float32)] * 2,
    )(mobility, indices, labels, order_late, adjoint_late)
    on_chip = pl.BlockSpec(memory_space=pltpu.VMEM)
    order_next, adjoint_order = pl.pallas_call(
        final_kernel,
        grid_spec=scalars(num_scalar_prefetch=1, grid=(count,), in_specs=[block, block, on_chip, on_chip, block, block], out_specs=[block, block]),
        out_shape=[jax.ShapeDtypeStruct(order_field.shape, jnp.float32)] * 2,
    )(mobility, order_field, adjoint_next, *[pltpu.with_memory_space_constraint(x, pltpu.VMEM) for x in (own, other)],
      inner_order, inner_adjoint)
    row = pl.BlockSpec((count, 1, depth, width), lambda s, *_: (0, s * (rows - 1), 0, 0))
    return pl.pallas_call(
        edge_kernel,
        grid_spec=scalars(num_scalar_prefetch=1, grid=(2,), in_specs=[on_chip, on_chip, row, row], out_specs=[row, row]),
        out_shape=[jax.ShapeDtypeStruct(order_field.shape, jnp.float32)] * 2,
        input_output_aliases={3: 0, 4: 1},
    )(mobility, *[pltpu.with_memory_space_constraint(x, pltpu.VMEM) for x in (below, above)], order_next, adjoint_order)


def solution(mesh):
    placed = (P("op", "space", None, None), P("op", "space", None, None), P("op"), P("space", None))
    return jax.shard_map(
        local,
        mesh=mesh,
        in_specs=placed,
        out_specs=(P("op", "space", None, None), P("op", "space", None, None)),
        check_vma=False,
    )
```

```python
import jax
import jax.numpy as jnp
from jax import lax
from jax.experimental import pallas as pl
from jax.experimental.pallas import tpu as pltpu
from jax.sharding import PartitionSpec as P


def shift_along(cells, axis, step):
    count = lax.axis_size(axis)
    return lax.ppermute(cells, axis, [(i, (i + step) % count) for i in range(count)])


def stencil(depth, width):
    level = lax.broadcasted_iota(jnp.int32, (depth, width), 0)
    top = level == depth - 1
    bottom = level == 0

    def laplace(centre, beside):
        beside = beside + pltpu.roll(centre, 1, 1) + pltpu.roll(centre, width - 1, 1)
        upper = jnp.where(top, centre, pltpu.roll(centre, depth - 1, 0))
        lower = jnp.where(bottom, centre, pltpu.roll(centre, 1, 0))
        return beside + upper + lower - 6.0 * centre

    return laplace


def inner_kernel(rate_ref, index_ref, labels_ref, order_ref, adjoint_ref, inner_order_ref, inner_adjoint_ref):
    p = pl.program_id(0)
    rate = 0.1 * rate_ref[p]
    index = index_ref[p]
    _, rows, depth, width = order_ref.shape
    laplace = stencil(depth, width)

    def load(j):
        return order_ref[0, j], rate * adjoint_ref[0, j]

    prev = None
    cur = load(0)
    for j in range(rows):
        nxt = load(j + 1) if j + 1 < rows else None
        o, w = cur
        if prev is None:
            beside = nxt
        elif nxt is None:
            beside = prev
        else:
            beside = (prev[0] + nxt[0], prev[1] + nxt[1])
        sign = jnp.where(labels_ref[j : j + 1, :] != index, 1.0, -1.0)
        inner_order_ref[0, j] = sign * o - 2.0 * (o * o * o) - 0.5 * laplace(o, beside[0])
        inner_adjoint_ref[0, j] = (sign - 6.0 * o * o) * w - 0.5 * laplace(w, beside[1])
        prev, cur = cur, nxt


def final_kernel(rate_ref, order_ref, adjoint_ref, own_ref, other_ref, inner_order_ref, inner_adjoint_ref,
                 order_next_ref, adjoint_order_ref):
    p = pl.program_id(0)
    rate = 0.1 * rate_ref[p]
    rows = order_ref.shape[1]
    for j in range(rows):
        o = order_ref[0, j]
        adj = adjoint_ref[0, j]
        w = rate * adj
        squares = 3.0 * (own_ref[0, j] + other_ref[0, j])
        coupled = 6.0 * (own_ref[1, j] + other_ref[1, j])
        order_next_ref[0, j] = o - rate * (inner_order_ref[0, j] + o * squares)
        adjoint_order_ref[0, j] = adj - ((inner_adjoint_ref[0, j] + w * squares) + o * coupled)


def edge_kernel(rate_ref, below_ref, above_ref, order_next_in, adjoint_order_in, order_next_ref, adjoint_order_ref,
                rows_buf, load_sem, store_sem):
    count, rows = order_next_in.shape[:2]
    sides = (0, rows - 1)
    loads = []
    for a, source in enumerate((order_next_in, adjoint_order_in)):
        for s, r in enumerate(sides):
            copy = pltpu.make_async_copy(source.at[:, pl.ds(r, 1)], rows_buf.at[a, s], load_sem.at[a, s])
            copy.start()
            loads.append(copy)
    for copy in loads:
        copy.wait()
    for s, halo in enumerate((below_ref, above_ref)):
        for p in range(count):
            rate = 0.1 * rate_ref[p]
            rows_buf[0, s, p, 0] = rows_buf[0, s, p, 0] + (0.5 * rate) * halo[0, p, 0]
            rows_buf[1, s, p, 0] = rows_buf[1, s, p, 0] + 0.5 * (rate * halo[1, p, 0])
    stores = []
    for a, target in enumerate((order_next_ref, adjoint_order_ref)):
        for s, r in enumerate(sides):
            copy = pltpu.make_async_copy(rows_buf.at[a, s], target.at[:, pl.ds(r, 1)], store_sem.at[a, s])
            copy.start()
            stores.append(copy)
    for copy in stores:
        copy.wait()


def local(order_field, adjoint_next, mobility, labels):
    count, rows, depth, width = order_field.shape
    first = lax.axis_index("op") * count
    indices = first + jnp.arange(count, dtype=jnp.int32)
    rates = mobility[:, None, None, None]
    weighted = 0.1 * rates * adjoint_next
    own = jnp.stack([jnp.sum(order_field * order_field, axis=0), jnp.sum(order_field * weighted, axis=0)])
    other = shift_along(own, "op", 1)
    pair = jnp.stack([order_field, adjoint_next])
    edges = jnp.concatenate([pair[:, :, :1], pair[:, :, -1:]], axis=2)
    edges, own, order_late, adjoint_late = lax.optimization_barrier((edges, own, order_field, adjoint_next))
    below = shift_along(edges[:, :, 1:], "space", 1)
    above = shift_along(edges[:, :, :1], "space", -1)
    scalars = pltpu.PrefetchScalarGridSpec
    block = pl.BlockSpec((1, rows, depth, width), lambda p, *_: (p, 0, 0, 0))
    plane = pl.BlockSpec((rows, width), lambda p, *_: (0, 0))
    inner_order, inner_adjoint = pl.pallas_call(
        inner_kernel,
        grid_spec=scalars(num_scalar_prefetch=2, grid=(count,), in_specs=[plane, block, block], out_specs=[block, block]),
        out_shape=[jax.ShapeDtypeStruct(order_field.shape, jnp.float32)] * 2,
    )(mobility, indices, labels, order_late, adjoint_late)
    on_chip = pl.BlockSpec(memory_space=pltpu.VMEM)
    order_next, adjoint_order = pl.pallas_call(
        final_kernel,
        grid_spec=scalars(num_scalar_prefetch=1, grid=(count,), in_specs=[block, block, on_chip, on_chip, block, block], out_specs=[block, block]),
        out_shape=[jax.ShapeDtypeStruct(order_field.shape, jnp.float32)] * 2,
    )(mobility, order_field, adjoint_next, *[pltpu.with_memory_space_constraint(x, pltpu.VMEM) for x in (own, other)],
      inner_order, inner_adjoint)
    anywhere = pl.BlockSpec(memory_space=pl.ANY)
    return pl.pallas_call(
        edge_kernel,
        in_specs=[pl.BlockSpec(memory_space=pltpu.SMEM), on_chip, on_chip, anywhere, anywhere],
        out_specs=[anywhere, anywhere],
        out_shape=[jax.ShapeDtypeStruct(order_field.shape, jnp.float32)] * 2,
        scratch_shapes=[
            pltpu.VMEM((2, 2, count, 1, depth, width), jnp.float32),
            pltpu.SemaphoreType.DMA((2, 2)),
            pltpu.SemaphoreType.DMA((2, 2)),
        ],
        input_output_aliases={3: 0, 4: 1},
    )(mobility, *[pltpu.with_memory_space_constraint(x, pltpu.VMEM) for x in (below, above)], order_next, adjoint_order)


def solution(mesh):
    placed = (P("op", "space", None, None), P("op", "space", None, None), P("op"), P("space", None))
    return jax.shard_map(
        local,
        mesh=mesh,
        in_specs=placed,
        out_specs=(P("op", "space", None, None), P("op", "space", None, None)),
        check_vma=False,
    )
```

```python
import jax
import jax.numpy as jnp
from jax import lax
from jax.experimental import pallas as pl
from jax.experimental.pallas import tpu as pltpu
from jax.sharding import PartitionSpec as P


def shift_along(cells, axis, step):
    count = lax.axis_size(axis)
    return lax.ppermute(cells, axis, [(i, (i + step) % count) for i in range(count)])


def stencil(depth, width):
    level = lax.broadcasted_iota(jnp.int32, (depth, width), 0)
    top = level == depth - 1
    bottom = level == 0

    def laplace(centre, beside):
        beside = beside + pltpu.roll(centre, 1, 1) + pltpu.roll(centre, width - 1, 1)
        upper = jnp.where(top, centre, pltpu.roll(centre, depth - 1, 0))
        lower = jnp.where(bottom, centre, pltpu.roll(centre, 1, 0))
        return beside + upper + lower - 6.0 * centre

    return laplace


def inner_kernel(rate_ref, index_ref, labels_ref, order_ref, adjoint_ref, inner_order_ref, inner_adjoint_ref):
    p = pl.program_id(0)
    rate = 0.1 * rate_ref[p]
    index = index_ref[p]
    _, rows, depth, width = order_ref.shape
    laplace = stencil(depth, width)

    def load(j):
        return order_ref[0, j], rate * adjoint_ref[0, j]

    prev = None
    cur = load(0)
    for j in range(rows):
        nxt = load(j + 1) if j + 1 < rows else None
        o, w = cur
        if prev is None:
            beside = nxt
        elif nxt is None:
            beside = prev
        else:
            beside = (prev[0] + nxt[0], prev[1] + nxt[1])
        sign = jnp.where(labels_ref[j : j + 1, :] != index, 1.0, -1.0)
        inner_order_ref[0, j] = sign * o - 2.0 * (o * o * o) - 0.5 * laplace(o, beside[0])
        inner_adjoint_ref[0, j] = (sign - 6.0 * o * o) * w - 0.5 * laplace(w, beside[1])
        prev, cur = cur, nxt


def final_kernel(rate_ref, order_ref, adjoint_ref, own_ref, other_ref, inner_order_ref, inner_adjoint_ref, *refs):
    order_next_ref, adjoint_order_ref = refs[-2:]
    p = pl.program_id(0)
    rate = 0.1 * rate_ref[p]
    rows = order_ref.shape[1]
    for j in range(rows):
        o = order_ref[0, j]
        adj = adjoint_ref[0, j]
        w = rate * adj
        squares = 3.0 * (own_ref[0, j] + other_ref[0, j])
        coupled = 6.0 * (own_ref[1, j] + other_ref[1, j])
        order_next_ref[0, j] = o - rate * (inner_order_ref[0, j] + o * squares)
        adjoint_order_ref[0, j] = adj - ((inner_adjoint_ref[0, j] + w * squares) + o * coupled)


def edge_kernel(rate_ref, below_ref, above_ref, order_next_in, adjoint_order_in, order_next_ref, adjoint_order_ref):
    side = pl.program_id(0)
    count = order_next_in.shape[0]
    for p in range(count):
        rate = 0.1 * rate_ref[p]
        order_row = jnp.where(side == 0, below_ref[0, p, 0], above_ref[0, p, 0])
        adjoint_row = jnp.where(side == 0, below_ref[1, p, 0], above_ref[1, p, 0])
        order_next_ref[p, 0] = order_next_in[p, 0] + (0.5 * rate) * order_row
        adjoint_order_ref[p, 0] = adjoint_order_in[p, 0] + 0.5 * (rate * adjoint_row)


def local(order_field, adjoint_next, mobility, labels):
    count, rows, depth, width = order_field.shape
    first = lax.axis_index("op") * count
    indices = first + jnp.arange(count, dtype=jnp.int32)
    rates = mobility[:, None, None, None]
    weighted = 0.1 * rates * adjoint_next
    half = rows // 2
    own = jnp.stack([jnp.sum(order_field * order_field, axis=0), jnp.sum(order_field * weighted, axis=0)])
    owns = [own[:, :half], own[:, half:]]
    others = [shift_along(own, "op", 1) for own in owns]
    pair = jnp.stack([order_field, adjoint_next])
    edges = jnp.concatenate([pair[:, :, :1], pair[:, :, -1:]], axis=2)
    edges, owns, order_late, adjoint_late = lax.optimization_barrier((edges, owns, order_field, adjoint_next))
    below = shift_along(edges[:, :, 1:], "space", 1)
    above = shift_along(edges[:, :, :1], "space", -1)
    scalars = pltpu.PrefetchScalarGridSpec
    block = pl.BlockSpec((1, rows, depth, width), lambda p, *_: (p, 0, 0, 0))
    plane = pl.BlockSpec((rows, width), lambda p, *_: (0, 0))
    inner_order, inner_adjoint = pl.pallas_call(
        inner_kernel,
        grid_spec=scalars(num_scalar_prefetch=2, grid=(count,), in_specs=[plane, block, block], out_specs=[block, block]),
        out_shape=[jax.ShapeDtypeStruct(order_field.shape, jnp.float32)] * 2,
    )(mobility, indices, labels, order_late, adjoint_late)
    on_chip = pl.BlockSpec(memory_space=pltpu.VMEM)
    cells = jax.ShapeDtypeStruct(order_field.shape, jnp.float32)
    outputs = []
    for h in range(2):
        part = pl.BlockSpec((1, half, depth, width), lambda p, *_, h=h: (p, h, 0, 0))
        extra = {}
        if outputs:
            extra = dict(input_output_aliases={7: 0, 8: 1})
        outputs = pl.pallas_call(
            final_kernel,
            grid_spec=scalars(
                num_scalar_prefetch=1,
                grid=(count,),
                in_specs=[part, part, on_chip, on_chip, part, part] + [pl.BlockSpec(memory_space=pl.ANY)] * len(outputs),
                out_specs=[part, part],
            ),
            out_shape=[cells, cells],
            **extra,
        )(mobility, order_field, adjoint_next, *[pltpu.with_memory_space_constraint(x, pltpu.VMEM) for x in (owns[h], others[h])],
          inner_order, inner_adjoint, *outputs)
    order_next, adjoint_order = outputs
    halo = pl.BlockSpec((2, count, 1, depth, width), lambda s, *_: (0, 0, 0, 0, 0))
    row = pl.BlockSpec((count, 1, depth, width), lambda s, *_: (0, s * (rows - 1), 0, 0))
    return pl.pallas_call(
        edge_kernel,
        grid_spec=scalars(
            num_scalar_prefetch=1, grid=(2,), in_specs=[on_chip, on_chip, row, row], out_specs=[row, row]
        ),
        out_shape=[cells, cells],
        input_output_aliases={3: 0, 4: 1},
    )(mobility, *[pltpu.with_memory_space_constraint(x, pltpu.VMEM) for x in (below, above)], order_next, adjoint_order)


def solution(mesh):
    placed = (P("op", "space", None, None), P("op", "space", None, None), P("op"), P("space", None))
    return jax.shard_map(
        local,
        mesh=mesh,
        in_specs=placed,
        out_specs=(P("op", "space", None, None), P("op", "space", None, None)),
        check_vma=False,
    )
```

```python
import jax
import jax.numpy as jnp
from jax import lax
from jax.experimental import pallas as pl
from jax.experimental.pallas import tpu as pltpu
from jax.sharding import PartitionSpec as P


def shift_along(cells, axis, step):
    count = lax.axis_size(axis)
    return lax.ppermute(cells, axis, [(i, (i + step) % count) for i in range(count)])


def stencil(depth, width):
    level = lax.broadcasted_iota(jnp.int32, (depth, width), 0)
    top = level == depth - 1
    bottom = level == 0

    def laplace(centre, beside):
        beside = beside + pltpu.roll(centre, 1, 1) + pltpu.roll(centre, width - 1, 1)
        upper = jnp.where(top, centre, pltpu.roll(centre, depth - 1, 0))
        lower = jnp.where(bottom, centre, pltpu.roll(centre, 1, 0))
        return beside + upper + lower - 6.0 * centre

    return laplace


def inner_kernel(rate_ref, index_ref, labels_ref, order_ref, adjoint_ref, inner_order_ref, inner_adjoint_ref):
    group = order_ref.shape[0]
    for q in range(group):
        inner_one(q, pl.program_id(0) * group + q, rate_ref, index_ref, labels_ref, order_ref, adjoint_ref,
                  inner_order_ref, inner_adjoint_ref)


def inner_one(q, p, rate_ref, index_ref, labels_ref, order_ref, adjoint_ref, inner_order_ref, inner_adjoint_ref):
    rate = 0.1 * rate_ref[p]
    index = index_ref[p]
    _, rows, depth, width = order_ref.shape
    laplace = stencil(depth, width)

    def load(j):
        return order_ref[q, j], rate * adjoint_ref[q, j]

    prev = None
    cur = load(0)
    for j in range(rows):
        nxt = load(j + 1) if j + 1 < rows else None
        o, w = cur
        if prev is None:
            beside = nxt
        elif nxt is None:
            beside = prev
        else:
            beside = (prev[0] + nxt[0], prev[1] + nxt[1])
        sign = jnp.where(labels_ref[j : j + 1, :] != index, 1.0, -1.0)
        inner_order_ref[q, j] = sign * o - 2.0 * (o * o * o) - 0.5 * laplace(o, beside[0])
        inner_adjoint_ref[q, j] = (sign - 6.0 * o * o) * w - 0.5 * laplace(w, beside[1])
        prev, cur = cur, nxt


def final_kernel(rate_ref, order_ref, adjoint_ref, own_ref, other_ref, inner_order_ref, inner_adjoint_ref,
                 order_next_ref, adjoint_order_ref):
    group, rows = order_ref.shape[:2]
    for q in range(group):
        final_one(q, pl.program_id(0) * group + q, rate_ref, order_ref, adjoint_ref, own_ref, other_ref,
                  inner_order_ref, inner_adjoint_ref, order_next_ref, adjoint_order_ref)


def final_one(q, p, rate_ref, order_ref, adjoint_ref, own_ref, other_ref, inner_order_ref, inner_adjoint_ref,
              order_next_ref, adjoint_order_ref):
    rate = 0.1 * rate_ref[p]
    rows = order_ref.shape[1]
    for j in range(rows):
        o = order_ref[q, j]
        adj = adjoint_ref[q, j]
        w = rate * adj
        squares = 3.0 * (own_ref[0, j] + other_ref[0, j])
        coupled = 6.0 * (own_ref[1, j] + other_ref[1, j])
        order_next_ref[q, j] = o - rate * (inner_order_ref[q, j] + o * squares)
        adjoint_order_ref[q, j] = adj - ((inner_adjoint_ref[q, j] + w * squares) + o * coupled)


def edge_kernel(rate_ref, below_ref, above_ref, order_next_in, adjoint_order_in, order_next_ref, adjoint_order_ref):
    side = pl.program_id(0)
    count = order_next_in.shape[0]
    for p in range(count):
        rate = 0.1 * rate_ref[p]
        order_row = jnp.where(side == 0, below_ref[0, p, 0], above_ref[0, p, 0])
        adjoint_row = jnp.where(side == 0, below_ref[1, p, 0], above_ref[1, p, 0])
        order_next_ref[p, 0] = order_next_in[p, 0] + (0.5 * rate) * order_row
        adjoint_order_ref[p, 0] = adjoint_order_in[p, 0] + 0.5 * (rate * adjoint_row)


def local(order_field, adjoint_next, mobility, labels):
    count, rows, depth, width = order_field.shape
    first = lax.axis_index("op") * count
    indices = first + jnp.arange(count, dtype=jnp.int32)
    rates = mobility[:, None, None, None]
    weighted = 0.1 * rates * adjoint_next
    own = jnp.stack([jnp.sum(order_field * order_field, axis=0), jnp.sum(order_field * weighted, axis=0)])
    other = shift_along(own, "op", 1)
    pair = jnp.stack([order_field, adjoint_next])
    edges = jnp.concatenate([pair[:, :, :1], pair[:, :, -1:]], axis=2)
    edges, own, order_late, adjoint_late = lax.optimization_barrier((edges, own, order_field, adjoint_next))
    below = shift_along(edges[:, :, 1:], "space", 1)
    above = shift_along(edges[:, :, :1], "space", -1)
    scalars = pltpu.PrefetchScalarGridSpec
    group = 2
    block = pl.BlockSpec((group, rows, depth, width), lambda p, *_: (p, 0, 0, 0))
    plane = pl.BlockSpec((rows, width), lambda p, *_: (0, 0))
    inner_order, inner_adjoint = pl.pallas_call(
        inner_kernel,
        grid_spec=scalars(num_scalar_prefetch=2, grid=(count // group,), in_specs=[plane, block, block], out_specs=[block, block]),
        out_shape=[jax.ShapeDtypeStruct(order_field.shape, jnp.float32)] * 2,
    )(mobility, indices, labels, order_late, adjoint_late)
    on_chip = pl.BlockSpec(memory_space=pltpu.VMEM)
    order_next, adjoint_order = pl.pallas_call(
        final_kernel,
        grid_spec=scalars(num_scalar_prefetch=1, grid=(count // group,), in_specs=[block, block, on_chip, on_chip, block, block], out_specs=[block, block]),
        out_shape=[jax.ShapeDtypeStruct(order_field.shape, jnp.float32)] * 2,
    )(mobility, order_field, adjoint_next, *[pltpu.with_memory_space_constraint(x, pltpu.VMEM) for x in (own, other)],
      inner_order, inner_adjoint)
    row = pl.BlockSpec((count, 1, depth, width), lambda s, *_: (0, s * (rows - 1), 0, 0))
    return pl.pallas_call(
        edge_kernel,
        grid_spec=scalars(num_scalar_prefetch=1, grid=(2,), in_specs=[on_chip, on_chip, row, row], out_specs=[row, row]),
        out_shape=[jax.ShapeDtypeStruct(order_field.shape, jnp.float32)] * 2,
        input_output_aliases={3: 0, 4: 1},
    )(mobility, *[pltpu.with_memory_space_constraint(x, pltpu.VMEM) for x in (below, above)], order_next, adjoint_order)


def solution(mesh):
    placed = (P("op", "space", None, None), P("op", "space", None, None), P("op"), P("space", None))
    return jax.shard_map(
        local,
        mesh=mesh,
        in_specs=placed,
        out_specs=(P("op", "space", None, None), P("op", "space", None, None)),
        check_vma=False,
    )
```

```python
import jax
import jax.numpy as jnp
from jax import lax
from jax.experimental import pallas as pl
from jax.experimental.pallas import tpu as pltpu
from jax.sharding import PartitionSpec as P


def shift_along(cells, axis, step):
    count = lax.axis_size(axis)
    return lax.ppermute(cells, axis, [(i, (i + step) % count) for i in range(count)])


def stencil(depth, width):
    level = lax.broadcasted_iota(jnp.int32, (depth, width), 0)
    top = level == depth - 1
    bottom = level == 0

    def laplace(centre, beside):
        beside = beside + pltpu.roll(centre, 1, 1) + pltpu.roll(centre, width - 1, 1)
        upper = jnp.where(top, centre, pltpu.roll(centre, depth - 1, 0))
        lower = jnp.where(bottom, centre, pltpu.roll(centre, 1, 0))
        return beside + upper + lower - 6.0 * centre

    return laplace


def inner_kernel(rate_ref, index_ref, labels_ref, order_ref, adjoint_ref, inner_order_ref, inner_adjoint_ref):
    group = order_ref.shape[0]
    for q in range(group):
        inner_one(q, pl.program_id(0) * group + q, rate_ref, index_ref, labels_ref, order_ref, adjoint_ref,
                  inner_order_ref, inner_adjoint_ref)


def inner_one(q, p, rate_ref, index_ref, labels_ref, order_ref, adjoint_ref, inner_order_ref, inner_adjoint_ref):
    rate = 0.1 * rate_ref[p]
    index = index_ref[p]
    _, rows, depth, width = order_ref.shape
    laplace = stencil(depth, width)

    def load(j):
        return order_ref[q, j], rate * adjoint_ref[q, j]

    prev = None
    cur = load(0)
    for j in range(rows):
        nxt = load(j + 1) if j + 1 < rows else None
        o, w = cur
        if prev is None:
            beside = nxt
        elif nxt is None:
            beside = prev
        else:
            beside = (prev[0] + nxt[0], prev[1] + nxt[1])
        sign = jnp.where(labels_ref[j : j + 1, :] != index, 1.0, -1.0)
        inner_order_ref[q, j] = sign * o - 2.0 * (o * o * o) - 0.5 * laplace(o, beside[0])
        inner_adjoint_ref[q, j] = (sign - 6.0 * o * o) * w - 0.5 * laplace(w, beside[1])
        prev, cur = cur, nxt


def final_kernel(rate_ref, order_ref, adjoint_ref, own_ref, other_ref, inner_order_ref, inner_adjoint_ref,
                 order_next_ref, adjoint_order_ref):
    group, rows = order_ref.shape[:2]
    for q in range(group):
        final_one(q, pl.program_id(0) * group + q, rate_ref, order_ref, adjoint_ref, own_ref, other_ref,
                  inner_order_ref, inner_adjoint_ref, order_next_ref, adjoint_order_ref)


def final_one(q, p, rate_ref, order_ref, adjoint_ref, own_ref, other_ref, inner_order_ref, inner_adjoint_ref,
              order_next_ref, adjoint_order_ref):
    rate = 0.1 * rate_ref[p]
    rows = order_ref.shape[1]
    for j in range(rows):
        o = order_ref[q, j]
        adj = adjoint_ref[q, j]
        w = rate * adj
        squares = 3.0 * (own_ref[0, j] + other_ref[0, j])
        coupled = 6.0 * (own_ref[1, j] + other_ref[1, j])
        order_next_ref[q, j] = o - rate * (inner_order_ref[q, j] + o * squares)
        adjoint_order_ref[q, j] = adj - ((inner_adjoint_ref[q, j] + w * squares) + o * coupled)


def edge_kernel(rate_ref, below_ref, above_ref, order_next_in, adjoint_order_in, order_next_ref, adjoint_order_ref):
    side = pl.program_id(0)
    count = order_next_in.shape[0]
    for p in range(count):
        rate = 0.1 * rate_ref[p]
        order_row = jnp.where(side == 0, below_ref[0, p, 0], above_ref[0, p, 0])
        adjoint_row = jnp.where(side == 0, below_ref[1, p, 0], above_ref[1, p, 0])
        order_next_ref[p, 0] = order_next_in[p, 0] + (0.5 * rate) * order_row
        adjoint_order_ref[p, 0] = adjoint_order_in[p, 0] + 0.5 * (rate * adjoint_row)


def local(order_field, adjoint_next, mobility, labels):
    count, rows, depth, width = order_field.shape
    first = lax.axis_index("op") * count
    indices = first + jnp.arange(count, dtype=jnp.int32)
    rates = mobility[:, None, None, None]
    weighted = 0.1 * rates * adjoint_next
    own = jnp.stack([jnp.sum(order_field * order_field, axis=0), jnp.sum(order_field * weighted, axis=0)])
    other = shift_along(own, "op", 1)
    pair = jnp.stack([order_field, adjoint_next])
    edges = jnp.concatenate([pair[:, :, :1], pair[:, :, -1:]], axis=2)
    edges, own, order_late, adjoint_late = lax.optimization_barrier((edges, own, order_field, adjoint_next))
    below = shift_along(edges[:, :, 1:], "space", 1)
    above = shift_along(edges[:, :, :1], "space", -1)
    scalars = pltpu.PrefetchScalarGridSpec
    group = 4
    block = pl.BlockSpec((group, rows, depth, width), lambda p, *_: (p, 0, 0, 0))
    plane = pl.BlockSpec((rows, width), lambda p, *_: (0, 0))
    inner_order, inner_adjoint = pl.pallas_call(
        inner_kernel,
        grid_spec=scalars(num_scalar_prefetch=2, grid=(count // group,), in_specs=[plane, block, block], out_specs=[block, block]),
        out_shape=[jax.ShapeDtypeStruct(order_field.shape, jnp.float32)] * 2,
    )(mobility, indices, labels, order_late, adjoint_late)
    on_chip = pl.BlockSpec(memory_space=pltpu.VMEM)
    order_next, adjoint_order = pl.pallas_call(
        final_kernel,
        grid_spec=scalars(num_scalar_prefetch=1, grid=(count // group,), in_specs=[block, block, on_chip, on_chip, block, block], out_specs=[block, block]),
        out_shape=[jax.ShapeDtypeStruct(order_field.shape, jnp.float32)] * 2,
    )(mobility, order_field, adjoint_next, *[pltpu.with_memory_space_constraint(x, pltpu.VMEM) for x in (own, other)],
      inner_order, inner_adjoint)
    row = pl.BlockSpec((count, 1, depth, width), lambda s, *_: (0, s * (rows - 1), 0, 0))
    return pl.pallas_call(
        edge_kernel,
        grid_spec=scalars(num_scalar_prefetch=1, grid=(2,), in_specs=[on_chip, on_chip, row, row], out_specs=[row, row]),
        out_shape=[jax.ShapeDtypeStruct(order_field.shape, jnp.float32)] * 2,
        input_output_aliases={3: 0, 4: 1},
    )(mobility, *[pltpu.with_memory_space_constraint(x, pltpu.VMEM) for x in (below, above)], order_next, adjoint_order)


def solution(mesh):
    placed = (P("op", "space", None, None), P("op", "space", None, None), P("op"), P("space", None))
    return jax.shard_map(
        local,
        mesh=mesh,
        in_specs=placed,
        out_specs=(P("op", "space", None, None), P("op", "space", None, None)),
        check_vma=False,
    )
```

```python
import jax
import jax.numpy as jnp
from jax import lax
from jax.experimental import pallas as pl
from jax.experimental.pallas import tpu as pltpu
from jax.sharding import PartitionSpec as P


def shift_along(cells, axis, step):
    count = lax.axis_size(axis)
    return lax.ppermute(cells, axis, [(i, (i + step) % count) for i in range(count)])


def stencil(depth, width):
    level = lax.broadcasted_iota(jnp.int32, (depth, width), 0)
    top = level == depth - 1
    bottom = level == 0

    def laplace(centre, beside):
        beside = beside + pltpu.roll(centre, 1, 1) + pltpu.roll(centre, width - 1, 1)
        upper = jnp.where(top, centre, pltpu.roll(centre, depth - 1, 0))
        lower = jnp.where(bottom, centre, pltpu.roll(centre, 1, 0))
        return beside + upper + lower - 6.0 * centre

    return laplace


def inner_kernel(rate_ref, index_ref, labels_ref, order_ref, adjoint_ref, inner_order_ref, inner_adjoint_ref):
    group = order_ref.shape[0]
    for q in range(group):
        inner_one(q, pl.program_id(0) * group + q, rate_ref, index_ref, labels_ref, order_ref, adjoint_ref,
                  inner_order_ref, inner_adjoint_ref)


def inner_one(q, p, rate_ref, index_ref, labels_ref, order_ref, adjoint_ref, inner_order_ref, inner_adjoint_ref):
    rate = 0.1 * rate_ref[p]
    index = index_ref[p]
    _, rows, depth, width = order_ref.shape
    laplace = stencil(depth, width)

    def load(j):
        return order_ref[q, j], rate * adjoint_ref[q, j]

    prev = None
    cur = load(0)
    for j in range(rows):
        nxt = load(j + 1) if j + 1 < rows else None
        o, w = cur
        if prev is None:
            beside = nxt
        elif nxt is None:
            beside = prev
        else:
            beside = (prev[0] + nxt[0], prev[1] + nxt[1])
        sign = jnp.where(labels_ref[j : j + 1, :] != index, 1.0, -1.0)
        inner_order_ref[q, j] = sign * o - 2.0 * (o * o * o) - 0.5 * laplace(o, beside[0])
        inner_adjoint_ref[q, j] = (sign - 6.0 * o * o) * w - 0.5 * laplace(w, beside[1])
        prev, cur = cur, nxt


def final_kernel(rate_ref, order_ref, adjoint_ref, own_ref, other_ref, inner_order_ref, inner_adjoint_ref,
                 order_next_ref, adjoint_order_ref, edge_ref):
    group, rows = order_ref.shape[:2]
    for q in range(group):
        p = pl.program_id(0) * group + q
        final_one(q, p, rate_ref, order_ref, adjoint_ref, own_ref, other_ref,
                  inner_order_ref, inner_adjoint_ref, order_next_ref, adjoint_order_ref)
        for s, r in enumerate((0, rows - 1)):
            edge_ref[0, s, p] = order_next_ref[q, r]
            edge_ref[1, s, p] = adjoint_order_ref[q, r]


def final_one(q, p, rate_ref, order_ref, adjoint_ref, own_ref, other_ref, inner_order_ref, inner_adjoint_ref,
              order_next_ref, adjoint_order_ref):
    rate = 0.1 * rate_ref[p]
    rows = order_ref.shape[1]
    for j in range(rows):
        o = order_ref[q, j]
        adj = adjoint_ref[q, j]
        w = rate * adj
        squares = 3.0 * (own_ref[0, j] + other_ref[0, j])
        coupled = 6.0 * (own_ref[1, j] + other_ref[1, j])
        order_next_ref[q, j] = o - rate * (inner_order_ref[q, j] + o * squares)
        adjoint_order_ref[q, j] = adj - ((inner_adjoint_ref[q, j] + w * squares) + o * coupled)


def edge_kernel(rate_ref, below_ref, above_ref, edge_ref, order_next_in, adjoint_order_in, order_next_ref, adjoint_order_ref,
                rows_buf, store_sem):
    count, rows = order_next_in.shape[:2]
    for s, halo in enumerate((below_ref, above_ref)):
        for p in range(count):
            rate = 0.1 * rate_ref[p]
            rows_buf[0, s, p, 0] = edge_ref[0, s, p] + (0.5 * rate) * halo[0, p, 0]
            rows_buf[1, s, p, 0] = edge_ref[1, s, p] + 0.5 * (rate * halo[1, p, 0])
    stores = []
    for a, target in enumerate((order_next_ref, adjoint_order_ref)):
        for s, r in enumerate((0, rows - 1)):
            copy = pltpu.make_async_copy(rows_buf.at[a, s], target.at[:, pl.ds(r, 1)], store_sem.at[a, s])
            copy.start()
            stores.append(copy)
    for copy in stores:
        copy.wait()


def local(order_field, adjoint_next, mobility, labels):
    count, rows, depth, width = order_field.shape
    first = lax.axis_index("op") * count
    indices = first + jnp.arange(count, dtype=jnp.int32)
    rates = mobility[:, None, None, None]
    weighted = 0.1 * rates * adjoint_next
    own = jnp.stack([jnp.sum(order_field * order_field, axis=0), jnp.sum(order_field * weighted, axis=0)])
    other = shift_along(own, "op", 1)
    pair = jnp.stack([order_field, adjoint_next])
    edges = jnp.concatenate([pair[:, :, :1], pair[:, :, -1:]], axis=2)
    edges, own, order_late, adjoint_late = lax.optimization_barrier((edges, own, order_field, adjoint_next))
    below = shift_along(edges[:, :, 1:], "space", 1)
    above = shift_along(edges[:, :, :1], "space", -1)
    scalars = pltpu.PrefetchScalarGridSpec
    group = 4
    block = pl.BlockSpec((group, rows, depth, width), lambda p, *_: (p, 0, 0, 0))
    plane = pl.BlockSpec((rows, width), lambda p, *_: (0, 0))
    inner_order, inner_adjoint = pl.pallas_call(
        inner_kernel,
        grid_spec=scalars(num_scalar_prefetch=2, grid=(count // group,), in_specs=[plane, block, block], out_specs=[block, block]),
        out_shape=[jax.ShapeDtypeStruct(order_field.shape, jnp.float32)] * 2,
    )(mobility, indices, labels, order_late, adjoint_late)
    on_chip = pl.BlockSpec(memory_space=pltpu.VMEM)
    whole = pl.BlockSpec((2, rows, depth, width), lambda p, *_: (0, 0, 0, 0))
    order_next, adjoint_order, edge_rows = pl.pallas_call(
        final_kernel,
        grid_spec=scalars(
            num_scalar_prefetch=1,
            grid=(count // group,),
            in_specs=[block, block, whole, whole, block, block],
            out_specs=[block, block, on_chip],
        ),
        out_shape=[jax.ShapeDtypeStruct(order_field.shape, jnp.float32)] * 2
        + [pltpu.VMEM((2, 2, count, depth, width), jnp.float32)],
    )(mobility, order_field, adjoint_next, own, other,
      inner_order, inner_adjoint)
    anywhere = pl.BlockSpec(memory_space=pl.ANY)
    return pl.pallas_call(
        edge_kernel,
        in_specs=[pl.BlockSpec(memory_space=pltpu.SMEM), on_chip, on_chip, on_chip, anywhere, anywhere],
        out_specs=[anywhere, anywhere],
        out_shape=[jax.ShapeDtypeStruct(order_field.shape, jnp.float32)] * 2,
        scratch_shapes=[pltpu.VMEM((2, 2, count, 1, depth, width), jnp.float32), pltpu.SemaphoreType.DMA((2, 2))],
        input_output_aliases={4: 0, 5: 1},
    )(mobility, *[pltpu.with_memory_space_constraint(x, pltpu.VMEM) for x in (below, above, edge_rows)], order_next, adjoint_order)


def solution(mesh):
    placed = (P("op", "space", None, None), P("op", "space", None, None), P("op"), P("space", None))
    return jax.shard_map(
        local,
        mesh=mesh,
        in_specs=placed,
        out_specs=(P("op", "space", None, None), P("op", "space", None, None)),
        check_vma=False,
    )
```

```python
import jax
import jax.numpy as jnp
from jax import lax
from jax.experimental import pallas as pl
from jax.experimental.pallas import tpu as pltpu
from jax.sharding import PartitionSpec as P


def shift_along(cells, axis, step):
    count = lax.axis_size(axis)
    return lax.ppermute(cells, axis, [(i, (i + step) % count) for i in range(count)])


def stencil(depth, width):
    level = lax.broadcasted_iota(jnp.int32, (depth, width), 0)
    top = level == depth - 1
    bottom = level == 0

    def laplace(centre, beside):
        beside = beside + pltpu.roll(centre, 1, 1) + pltpu.roll(centre, width - 1, 1)
        upper = jnp.where(top, centre, pltpu.roll(centre, depth - 1, 0))
        lower = jnp.where(bottom, centre, pltpu.roll(centre, 1, 0))
        return beside + upper + lower - 6.0 * centre

    return laplace


def inner_kernel(rate_ref, index_ref, labels_ref, order_ref, adjoint_ref, inner_order_ref, inner_adjoint_ref):
    group = order_ref.shape[0]
    for q in range(group):
        inner_one(q, pl.program_id(0) * group + q, rate_ref, index_ref, labels_ref, order_ref, adjoint_ref,
                  inner_order_ref, inner_adjoint_ref)


def inner_one(q, p, rate_ref, index_ref, labels_ref, order_ref, adjoint_ref, inner_order_ref, inner_adjoint_ref):
    rate = 0.1 * rate_ref[p]
    index = index_ref[p]
    _, rows, depth, width = order_ref.shape
    laplace = stencil(depth, width)

    def load(j):
        return order_ref[q, j], rate * adjoint_ref[q, j]

    prev = None
    cur = load(0)
    for j in range(rows):
        nxt = load(j + 1) if j + 1 < rows else None
        o, w = cur
        if prev is None:
            beside = nxt
        elif nxt is None:
            beside = prev
        else:
            beside = (prev[0] + nxt[0], prev[1] + nxt[1])
        sign = jnp.where(labels_ref[j : j + 1, :] != index, 1.0, -1.0)
        inner_order_ref[q, j] = sign * o - 2.0 * (o * o * o) - 0.5 * laplace(o, beside[0])
        inner_adjoint_ref[q, j] = (sign - 6.0 * o * o) * w - 0.5 * laplace(w, beside[1])
        prev, cur = cur, nxt


def final_kernel(rate_ref, order_ref, adjoint_ref, own_ref, other_ref, inner_order_ref, inner_adjoint_ref,
                 order_next_ref, adjoint_order_ref):
    group, rows = order_ref.shape[:2]
    for q in range(group):
        final_one(q, pl.program_id(0) * group + q, rate_ref, order_ref, adjoint_ref, own_ref, other_ref,
                  inner_order_ref, inner_adjoint_ref, order_next_ref, adjoint_order_ref)


def final_one(q, p, rate_ref, order_ref, adjoint_ref, own_ref, other_ref, inner_order_ref, inner_adjoint_ref,
              order_next_ref, adjoint_order_ref):
    rate = 0.1 * rate_ref[p]
    rows = order_ref.shape[1]
    for j in range(rows):
        o = order_ref[q, j]
        adj = adjoint_ref[q, j]
        w = rate * adj
        squares = 3.0 * (own_ref[0, j] + other_ref[0, j])
        coupled = 6.0 * (own_ref[1, j] + other_ref[1, j])
        order_next_ref[q, j] = o - rate * (inner_order_ref[q, j] + o * squares)
        adjoint_order_ref[q, j] = adj - ((inner_adjoint_ref[q, j] + w * squares) + o * coupled)


def edge_kernel(rate_ref, below_ref, above_ref, order_next_in, adjoint_order_in, order_next_ref, adjoint_order_ref):
    side = pl.program_id(0)
    count = order_next_in.shape[0]
    for p in range(count):
        rate = 0.1 * rate_ref[p]
        order_row = jnp.where(side == 0, below_ref[0, p, 0], above_ref[0, p, 0])
        adjoint_row = jnp.where(side == 0, below_ref[1, p, 0], above_ref[1, p, 0])
        order_next_ref[p, 0] = order_next_in[p, 0] + (0.5 * rate) * order_row
        adjoint_order_ref[p, 0] = adjoint_order_in[p, 0] + 0.5 * (rate * adjoint_row)


def local(order_field, adjoint_next, mobility, labels):
    count, rows, depth, width = order_field.shape
    first = lax.axis_index("op") * count
    indices = first + jnp.arange(count, dtype=jnp.int32)
    rates = mobility[:, None, None, None]
    weighted = 0.1 * rates * adjoint_next
    own = jnp.stack([jnp.sum(order_field * order_field, axis=0), jnp.sum(order_field * weighted, axis=0)])
    both = lax.all_to_all(jnp.stack([own, own]), "op", 0, 0, tiled=False)
    other = both[1 - lax.axis_index("op")]
    pair = jnp.stack([order_field, adjoint_next])
    edges = jnp.concatenate([pair[:, :, :1], pair[:, :, -1:]], axis=2)
    edges, own, order_late, adjoint_late = lax.optimization_barrier((edges, own, order_field, adjoint_next))
    below = shift_along(edges[:, :, 1:], "space", 1)
    above = shift_along(edges[:, :, :1], "space", -1)
    scalars = pltpu.PrefetchScalarGridSpec
    group = 4
    block = pl.BlockSpec((group, rows, depth, width), lambda p, *_: (p, 0, 0, 0))
    plane = pl.BlockSpec((rows, width), lambda p, *_: (0, 0))
    inner_order, inner_adjoint = pl.pallas_call(
        inner_kernel,
        grid_spec=scalars(num_scalar_prefetch=2, grid=(count // group,), in_specs=[plane, block, block], out_specs=[block, block]),
        out_shape=[jax.ShapeDtypeStruct(order_field.shape, jnp.float32)] * 2,
    )(mobility, indices, labels, order_late, adjoint_late)
    on_chip = pl.BlockSpec(memory_space=pltpu.VMEM)
    order_next, adjoint_order = pl.pallas_call(
        final_kernel,
        grid_spec=scalars(num_scalar_prefetch=1, grid=(count // group,), in_specs=[block, block, on_chip, on_chip, block, block], out_specs=[block, block]),
        out_shape=[jax.ShapeDtypeStruct(order_field.shape, jnp.float32)] * 2,
    )(mobility, order_field, adjoint_next, *[pltpu.with_memory_space_constraint(x, pltpu.VMEM) for x in (own, other)],
      inner_order, inner_adjoint)
    row = pl.BlockSpec((count, 1, depth, width), lambda s, *_: (0, s * (rows - 1), 0, 0))
    return pl.pallas_call(
        edge_kernel,
        grid_spec=scalars(num_scalar_prefetch=1, grid=(2,), in_specs=[on_chip, on_chip, row, row], out_specs=[row, row]),
        out_shape=[jax.ShapeDtypeStruct(order_field.shape, jnp.float32)] * 2,
        input_output_aliases={3: 0, 4: 1},
    )(mobility, *[pltpu.with_memory_space_constraint(x, pltpu.VMEM) for x in (below, above)], order_next, adjoint_order)


def solution(mesh):
    placed = (P("op", "space", None, None), P("op", "space", None, None), P("op"), P("space", None))
    return jax.shard_map(
        local,
        mesh=mesh,
        in_specs=placed,
        out_specs=(P("op", "space", None, None), P("op", "space", None, None)),
        check_vma=False,
    )
```

```python
import jax
import jax.numpy as jnp
from jax import lax
from jax.experimental import pallas as pl
from jax.experimental.pallas import tpu as pltpu
from jax.sharding import PartitionSpec as P


def shift_along(cells, axis, step):
    count = lax.axis_size(axis)
    return lax.ppermute(cells, axis, [(i, (i + step) % count) for i in range(count)])


def stencil(depth, width):
    level = lax.broadcasted_iota(jnp.int32, (depth, width), 0)
    top = level == depth - 1
    bottom = level == 0

    def laplace(centre, beside):
        beside = beside + pltpu.roll(centre, 1, 1) + pltpu.roll(centre, width - 1, 1)
        upper = jnp.where(top, centre, pltpu.roll(centre, depth - 1, 0))
        lower = jnp.where(bottom, centre, pltpu.roll(centre, 1, 0))
        return beside + upper + lower - 6.0 * centre

    return laplace


def inner_kernel(rate_ref, index_ref, labels_ref, order_ref, adjoint_ref, inner_order_ref, inner_adjoint_ref):
    group = order_ref.shape[0]
    for q in range(group):
        inner_one(q, pl.program_id(0) * group + q, rate_ref, index_ref, labels_ref, order_ref, adjoint_ref,
                  inner_order_ref, inner_adjoint_ref)


def inner_one(q, p, rate_ref, index_ref, labels_ref, order_ref, adjoint_ref, inner_order_ref, inner_adjoint_ref):
    rate = 0.1 * rate_ref[p]
    index = index_ref[p]
    _, rows, depth, width = order_ref.shape
    laplace = stencil(depth, width)

    def load(j):
        return order_ref[q, j], rate * adjoint_ref[q, j]

    prev = None
    cur = load(0)
    for j in range(rows):
        nxt = load(j + 1) if j + 1 < rows else None
        o, w = cur
        if prev is None:
            beside = nxt
        elif nxt is None:
            beside = prev
        else:
            beside = (prev[0] + nxt[0], prev[1] + nxt[1])
        sign = jnp.where(labels_ref[j : j + 1, :] != index, 1.0, -1.0)
        inner_order_ref[q, j] = sign * o - 2.0 * (o * o * o) - 0.5 * laplace(o, beside[0])
        inner_adjoint_ref[q, j] = (sign - 6.0 * o * o) * w - 0.5 * laplace(w, beside[1])
        prev, cur = cur, nxt


def final_kernel(rate_ref, order_ref, adjoint_ref, own_ref, other_ref, inner_order_ref, inner_adjoint_ref,
                 order_next_ref, adjoint_order_ref, edge_ref):
    group, rows = order_ref.shape[:2]
    for q in range(group):
        p = pl.program_id(0) * group + q
        final_one(q, p, rate_ref, order_ref, adjoint_ref, own_ref, other_ref,
                  inner_order_ref, inner_adjoint_ref, order_next_ref, adjoint_order_ref)
        for s, r in enumerate((0, rows - 1)):
            edge_ref[0, s, q] = order_next_ref[q, r]
            edge_ref[1, s, q] = adjoint_order_ref[q, r]


def final_one(q, p, rate_ref, order_ref, adjoint_ref, own_ref, other_ref, inner_order_ref, inner_adjoint_ref,
              order_next_ref, adjoint_order_ref):
    rate = 0.1 * rate_ref[p]
    rows = order_ref.shape[1]
    for j in range(rows):
        o = order_ref[q, j]
        adj = adjoint_ref[q, j]
        w = rate * adj
        squares = 3.0 * (own_ref[0, j] + other_ref[0, j])
        coupled = 6.0 * (own_ref[1, j] + other_ref[1, j])
        order_next_ref[q, j] = o - rate * (inner_order_ref[q, j] + o * squares)
        adjoint_order_ref[q, j] = adj - ((inner_adjoint_ref[q, j] + w * squares) + o * coupled)


def edge_kernel(rate_ref, below_ref, above_ref, edge_hbm, order_next_in, adjoint_order_in, order_next_ref, adjoint_order_ref,
                edge_ref, rows_buf, load_sem, store_sem):
    count, rows = order_next_in.shape[:2]
    load = pltpu.make_async_copy(edge_hbm, edge_ref, load_sem)
    load.start()
    load.wait()
    for s, halo in enumerate((below_ref, above_ref)):
        for p in range(count):
            rate = 0.1 * rate_ref[p]
            rows_buf[0, s, p, 0] = edge_ref[0, s, p] + (0.5 * rate) * halo[0, p, 0]
            rows_buf[1, s, p, 0] = edge_ref[1, s, p] + 0.5 * (rate * halo[1, p, 0])
    stores = []
    for a, target in enumerate((order_next_ref, adjoint_order_ref)):
        for s, r in enumerate((0, rows - 1)):
            copy = pltpu.make_async_copy(rows_buf.at[a, s], target.at[:, pl.ds(r, 1)], store_sem.at[a, s])
            copy.start()
            stores.append(copy)
    for copy in stores:
        copy.wait()


def local(order_field, adjoint_next, mobility, labels):
    count, rows, depth, width = order_field.shape
    first = lax.axis_index("op") * count
    indices = first + jnp.arange(count, dtype=jnp.int32)
    rates = mobility[:, None, None, None]
    weighted = 0.1 * rates * adjoint_next
    own = jnp.stack([jnp.sum(order_field * order_field, axis=0), jnp.sum(order_field * weighted, axis=0)])
    other = shift_along(own, "op", 1)
    pair = jnp.stack([order_field, adjoint_next])
    edges = jnp.concatenate([pair[:, :, :1], pair[:, :, -1:]], axis=2)
    edges, own, order_late, adjoint_late = lax.optimization_barrier((edges, own, order_field, adjoint_next))
    below = shift_along(edges[:, :, 1:], "space", 1)
    above = shift_along(edges[:, :, :1], "space", -1)
    scalars = pltpu.PrefetchScalarGridSpec
    group = 4
    block = pl.BlockSpec((group, rows, depth, width), lambda p, *_: (p, 0, 0, 0))
    plane = pl.BlockSpec((rows, width), lambda p, *_: (0, 0))
    inner_order, inner_adjoint = pl.pallas_call(
        inner_kernel,
        grid_spec=scalars(num_scalar_prefetch=2, grid=(count // group,), in_specs=[plane, block, block], out_specs=[block, block]),
        out_shape=[jax.ShapeDtypeStruct(order_field.shape, jnp.float32)] * 2,
    )(mobility, indices, labels, order_late, adjoint_late)
    on_chip = pl.BlockSpec(memory_space=pltpu.VMEM)
    order_next, adjoint_order, edge_rows = pl.pallas_call(
        final_kernel,
        grid_spec=scalars(
            num_scalar_prefetch=1,
            grid=(count // group,),
            in_specs=[block, block, on_chip, on_chip, block, block],
            out_specs=[block, block, pl.BlockSpec((2, 2, group, depth, width), lambda p, *_: (0, 0, p, 0, 0))],
        ),
        out_shape=[jax.ShapeDtypeStruct(order_field.shape, jnp.float32)] * 2
        + [jax.ShapeDtypeStruct((2, 2, count, depth, width), jnp.float32)],
    )(mobility, order_field, adjoint_next, *[pltpu.with_memory_space_constraint(x, pltpu.VMEM) for x in (own, other)],
      inner_order, inner_adjoint)
    anywhere = pl.BlockSpec(memory_space=pl.ANY)
    return pl.pallas_call(
        edge_kernel,
        in_specs=[pl.BlockSpec(memory_space=pltpu.SMEM), on_chip, on_chip, anywhere, anywhere, anywhere],
        out_specs=[anywhere, anywhere],
        out_shape=[jax.ShapeDtypeStruct(order_field.shape, jnp.float32)] * 2,
        scratch_shapes=[
            pltpu.VMEM((2, 2, count, depth, width), jnp.float32),
            pltpu.VMEM((2, 2, count, 1, depth, width), jnp.float32),
            pltpu.SemaphoreType.DMA(()),
            pltpu.SemaphoreType.DMA((2, 2)),
        ],
        input_output_aliases={4: 0, 5: 1},
    )(mobility, *[pltpu.with_memory_space_constraint(x, pltpu.VMEM) for x in (below, above)], edge_rows, order_next, adjoint_order)


def solution(mesh):
    placed = (P("op", "space", None, None), P("op", "space", None, None), P("op"), P("space", None))
    return jax.shard_map(
        local,
        mesh=mesh,
        in_specs=placed,
        out_specs=(P("op", "space", None, None), P("op", "space", None, None)),
        check_vma=False,
    )
```

```python
import jax
import jax.numpy as jnp
from jax import lax
from jax.experimental import pallas as pl
from jax.experimental.pallas import tpu as pltpu
from jax.sharding import PartitionSpec as P


def shift_along(cells, axis, step):
    count = lax.axis_size(axis)
    return lax.ppermute(cells, axis, [(i, (i + step) % count) for i in range(count)])


def stencil(depth, width):
    level = lax.broadcasted_iota(jnp.int32, (depth, width), 0)
    top = level == depth - 1
    bottom = level == 0

    def laplace(centre, beside):
        beside = beside + pltpu.roll(centre, 1, 1) + pltpu.roll(centre, width - 1, 1)
        upper = jnp.where(top, centre, pltpu.roll(centre, depth - 1, 0))
        lower = jnp.where(bottom, centre, pltpu.roll(centre, 1, 0))
        return beside + upper + lower - 6.0 * centre

    return laplace


def inner_kernel(rate_ref, index_ref, labels_ref, order_ref, adjoint_ref, inner_order_ref, inner_adjoint_ref):
    group = order_ref.shape[0]
    for q in range(group):
        inner_one(q, pl.program_id(0) * group + q, rate_ref, index_ref, labels_ref, order_ref, adjoint_ref,
                  inner_order_ref, inner_adjoint_ref)


def inner_one(q, p, rate_ref, index_ref, labels_ref, order_ref, adjoint_ref, inner_order_ref, inner_adjoint_ref):
    rate = 0.1 * rate_ref[p]
    index = index_ref[p]
    _, rows, depth, width = order_ref.shape
    laplace = stencil(depth, width)

    def load(j):
        return order_ref[q, j], rate * adjoint_ref[q, j]

    prev = None
    cur = load(0)
    for j in range(rows):
        nxt = load(j + 1) if j + 1 < rows else None
        o, w = cur
        if prev is None:
            beside = nxt
        elif nxt is None:
            beside = prev
        else:
            beside = (prev[0] + nxt[0], prev[1] + nxt[1])
        sign = jnp.where(labels_ref[j : j + 1, :] != index, 1.0, -1.0)
        inner_order_ref[q, j] = sign * o - 2.0 * (o * o * o) - 0.5 * laplace(o, beside[0])
        inner_adjoint_ref[q, j] = (sign - 6.0 * o * o) * w - 0.5 * laplace(w, beside[1])
        prev, cur = cur, nxt


def final_kernel(rate_ref, order_ref, adjoint_ref, own_ref, other_ref, inner_order_ref, inner_adjoint_ref,
                 order_next_ref, adjoint_order_ref):
    group, rows = order_ref.shape[:2]
    for q in range(group):
        final_one(q, pl.program_id(0) * group + q, rate_ref, order_ref, adjoint_ref, own_ref, other_ref,
                  inner_order_ref, inner_adjoint_ref, order_next_ref, adjoint_order_ref)


def final_one(q, p, rate_ref, order_ref, adjoint_ref, own_ref, other_ref, inner_order_ref, inner_adjoint_ref,
              order_next_ref, adjoint_order_ref):
    rate = 0.1 * rate_ref[p]
    rows = order_ref.shape[1]
    for j in range(rows):
        o = order_ref[q, j]
        adj = adjoint_ref[q, j]
        w = rate * adj
        squares = 3.0 * (own_ref[0, j] + other_ref[0, j])
        coupled = 6.0 * (own_ref[1, j] + other_ref[1, j])
        order_next_ref[q, j] = o - rate * (inner_order_ref[q, j] + o * squares)
        adjoint_order_ref[q, j] = adj - ((inner_adjoint_ref[q, j] + w * squares) + o * coupled)


def edge_kernel(rate_ref, below_ref, above_ref, order_next_in, adjoint_order_in, order_next_ref, adjoint_order_ref):
    side = pl.program_id(0)
    count = order_next_in.shape[0]
    for p in range(count):
        rate = 0.1 * rate_ref[p]
        order_row = jnp.where(side == 0, below_ref[0, p, 0], above_ref[0, p, 0])
        adjoint_row = jnp.where(side == 0, below_ref[1, p, 0], above_ref[1, p, 0])
        order_next_ref[p, 0] = order_next_in[p, 0] + (0.5 * rate) * order_row
        adjoint_order_ref[p, 0] = adjoint_order_in[p, 0] + 0.5 * (rate * adjoint_row)


def local(order_field, adjoint_next, mobility, labels):
    count, rows, depth, width = order_field.shape
    first = lax.axis_index("op") * count
    indices = first + jnp.arange(count, dtype=jnp.int32)
    rates = mobility[:, None, None, None]
    weighted = 0.1 * rates * adjoint_next
    own = jnp.stack([jnp.sum(order_field * order_field, axis=0), jnp.sum(order_field * weighted, axis=0)])
    other = shift_along(own, "op", 1)
    pair = jnp.stack([order_field, adjoint_next])
    edges = jnp.concatenate([pair[:, :, :1], pair[:, :, -1:]], axis=2)
    edges, own, order_late, adjoint_late = lax.optimization_barrier((edges, own, order_field, adjoint_next))
    below = shift_along(edges[:, :, 1:], "space", 1)
    above = shift_along(edges[:, :, :1], "space", -1)
    scalars = pltpu.PrefetchScalarGridSpec
    group = 4
    block = pl.BlockSpec((group, rows, depth, width), lambda p, *_: (p, 0, 0, 0))
    plane = pl.BlockSpec((rows, width), lambda p, *_: (0, 0))
    inner_order, inner_adjoint = pl.pallas_call(
        inner_kernel,
        grid_spec=scalars(num_scalar_prefetch=2, grid=(count // group,), in_specs=[plane, block, block], out_specs=[block, block]),
        out_shape=[jax.ShapeDtypeStruct(order_field.shape, jnp.float32)] * 2,
    )(mobility, indices, labels, order_late, adjoint_late)
    on_chip = pl.BlockSpec(memory_space=pltpu.VMEM)
    every = pl.BlockSpec((count, rows, depth, width), lambda p, *_: (0, 0, 0, 0))
    order_next, adjoint_order = pl.pallas_call(
        final_kernel,
        grid_spec=scalars(num_scalar_prefetch=1, grid=(1,), in_specs=[every, every, on_chip, on_chip, every, every], out_specs=[every, every]),
        out_shape=[jax.ShapeDtypeStruct(order_field.shape, jnp.float32)] * 2,
    )(mobility, order_field, adjoint_next, *[pltpu.with_memory_space_constraint(x, pltpu.VMEM) for x in (own, other)],
      inner_order, inner_adjoint)
    row = pl.BlockSpec((count, 1, depth, width), lambda s, *_: (0, s * (rows - 1), 0, 0))
    return pl.pallas_call(
        edge_kernel,
        grid_spec=scalars(num_scalar_prefetch=1, grid=(2,), in_specs=[on_chip, on_chip, row, row], out_specs=[row, row]),
        out_shape=[jax.ShapeDtypeStruct(order_field.shape, jnp.float32)] * 2,
        input_output_aliases={3: 0, 4: 1},
    )(mobility, *[pltpu.with_memory_space_constraint(x, pltpu.VMEM) for x in (below, above)], order_next, adjoint_order)


def solution(mesh):
    placed = (P("op", "space", None, None), P("op", "space", None, None), P("op"), P("space", None))
    return jax.shard_map(
        local,
        mesh=mesh,
        in_specs=placed,
        out_specs=(P("op", "space", None, None), P("op", "space", None, None)),
        check_vma=False,
    )
```

```python
import jax
import jax.numpy as jnp
from jax import lax
from jax.experimental import pallas as pl
from jax.experimental.pallas import tpu as pltpu
from jax.sharding import PartitionSpec as P


def shift_along(cells, axis, step):
    count = lax.axis_size(axis)
    return lax.ppermute(cells, axis, [(i, (i + step) % count) for i in range(count)])


def stencil(depth, width):
    level = lax.broadcasted_iota(jnp.int32, (depth, width), 0)
    top = level == depth - 1
    bottom = level == 0

    def laplace(centre, beside):
        beside = beside + pltpu.roll(centre, 1, 1) + pltpu.roll(centre, width - 1, 1)
        upper = jnp.where(top, centre, pltpu.roll(centre, depth - 1, 0))
        lower = jnp.where(bottom, centre, pltpu.roll(centre, 1, 0))
        return beside + upper + lower - 6.0 * centre

    return laplace


def inner_kernel(rate_ref, index_ref, labels_ref, order_ref, adjoint_ref, inner_order_ref, inner_adjoint_ref):
    group = order_ref.shape[0]
    for q in range(group):
        inner_one(q, pl.program_id(0) * group + q, rate_ref, index_ref, labels_ref, order_ref, adjoint_ref,
                  inner_order_ref, inner_adjoint_ref)


def inner_one(q, p, rate_ref, index_ref, labels_ref, order_ref, adjoint_ref, inner_order_ref, inner_adjoint_ref):
    rate = 0.1 * rate_ref[p]
    index = index_ref[p]
    _, rows, depth, width = order_ref.shape
    laplace = stencil(depth, width)

    def load(j):
        return order_ref[q, j], rate * adjoint_ref[q, j]

    prev = None
    cur = load(0)
    for j in range(rows):
        nxt = load(j + 1) if j + 1 < rows else None
        o, w = cur
        if prev is None:
            beside = nxt
        elif nxt is None:
            beside = prev
        else:
            beside = (prev[0] + nxt[0], prev[1] + nxt[1])
        sign = jnp.where(labels_ref[j : j + 1, :] != index, 1.0, -1.0)
        inner_order_ref[q, j] = sign * o - 2.0 * (o * o * o) - 0.5 * laplace(o, beside[0])
        inner_adjoint_ref[q, j] = (sign - 6.0 * o * o) * w - 0.5 * laplace(w, beside[1])
        prev, cur = cur, nxt


def final_kernel(rate_ref, order_ref, adjoint_ref, own_ref, other_ref, inner_order_ref, inner_adjoint_ref,
                 order_next_ref, adjoint_order_ref):
    group, rows = order_ref.shape[:2]
    for q in range(group):
        final_one(q, pl.program_id(0) * group + q, rate_ref, order_ref, adjoint_ref, own_ref, other_ref,
                  inner_order_ref, inner_adjoint_ref, order_next_ref, adjoint_order_ref)


def final_one(q, p, rate_ref, order_ref, adjoint_ref, own_ref, other_ref, inner_order_ref, inner_adjoint_ref,
              order_next_ref, adjoint_order_ref):
    rate = 0.1 * rate_ref[p]
    rows = order_ref.shape[1]
    for j in range(rows):
        o = order_ref[q, j]
        adj = adjoint_ref[q, j]
        w = rate * adj
        squares = 3.0 * (own_ref[0, j] + other_ref[0, j])
        coupled = 6.0 * (own_ref[1, j] + other_ref[1, j])
        order_next_ref[q, j] = o - rate * (inner_order_ref[q, j] + o * squares)
        adjoint_order_ref[q, j] = adj - ((inner_adjoint_ref[q, j] + w * squares) + o * coupled)


def edge_kernel(rate_ref, flag_ref, cross_ref, below_ref, above_ref, order_next_in, adjoint_order_in,
                order_next_ref, adjoint_order_ref):
    side = pl.program_id(0)
    count = order_next_in.shape[0]
    crossed = jnp.where(side == 0, flag_ref[0], flag_ref[1]) != 0
    for p in range(count):
        rate = 0.1 * rate_ref[p]
        order_row = jnp.where(side == 0, below_ref[0, p, 0], above_ref[0, p, 0])
        adjoint_row = jnp.where(side == 0, below_ref[1, p, 0], above_ref[1, p, 0])
        order_row = jnp.where(crossed, cross_ref[0, p, 0], order_row)
        adjoint_row = jnp.where(crossed, cross_ref[1, p, 0], adjoint_row)
        order_next_ref[p, 0] = order_next_in[p, 0] + (0.5 * rate) * order_row
        adjoint_order_ref[p, 0] = adjoint_order_in[p, 0] + 0.5 * (rate * adjoint_row)


def local(order_field, adjoint_next, mobility, labels):
    count, rows, depth, width = order_field.shape
    first = lax.axis_index("op") * count
    indices = first + jnp.arange(count, dtype=jnp.int32)
    pair = jnp.stack([order_field, adjoint_next])
    head = pair[:, :, :1]
    tail = pair[:, :, -1:]
    tiles = lax.axis_size("space")
    span = 32 if tiles % 32 == 0 else tiles
    where = lax.axis_index("space")
    opening = where % span == 0
    last = (where + 1) % span == 0
    crossing = [(i, (i + 1) % tiles) for i in range(tiles) if (i + 1) % span == 0]
    crossing += [(i, (i - 1) % tiles) for i in range(tiles) if i % span == 0]
    outgoing, order_sums, adjoint_sums = lax.optimization_barrier((jnp.where(last, tail, head), order_field, adjoint_next))
    cross = lax.ppermute(outgoing, "space", crossing)
    rates = mobility[:, None, None, None]
    weighted = 0.1 * rates * adjoint_sums
    own = jnp.stack([jnp.sum(order_sums * order_sums, axis=0), jnp.sum(order_sums * weighted, axis=0)])
    other = shift_along(own, "op", 1)
    edges = jnp.concatenate([head, tail], axis=2)
    edges, own, order_late, adjoint_late = lax.optimization_barrier((edges, own, order_field, adjoint_next))
    below = lax.ppermute(edges[:, :, 1:], "space", [(i, i + 1) for i in range(tiles - 1) if (i + 1) % span != 0])
    above = lax.ppermute(edges[:, :, :1], "space", [(i, i - 1) for i in range(1, tiles) if i % span != 0])
    flags = jnp.stack([opening, last]).astype(jnp.int32)
    scalars = pltpu.PrefetchScalarGridSpec
    group = 4
    block = pl.BlockSpec((group, rows, depth, width), lambda p, *_: (p, 0, 0, 0))
    plane = pl.BlockSpec((rows, width), lambda p, *_: (0, 0))
    inner_order, inner_adjoint = pl.pallas_call(
        inner_kernel,
        grid_spec=scalars(num_scalar_prefetch=2, grid=(count // group,), in_specs=[plane, block, block], out_specs=[block, block]),
        out_shape=[jax.ShapeDtypeStruct(order_field.shape, jnp.float32)] * 2,
    )(mobility, indices, labels, order_late, adjoint_late)
    on_chip = pl.BlockSpec(memory_space=pltpu.VMEM)
    order_next, adjoint_order = pl.pallas_call(
        final_kernel,
        grid_spec=scalars(num_scalar_prefetch=1, grid=(count // group,), in_specs=[block, block, on_chip, on_chip, block, block], out_specs=[block, block]),
        out_shape=[jax.ShapeDtypeStruct(order_field.shape, jnp.float32)] * 2,
    )(mobility, order_field, adjoint_next, *[pltpu.with_memory_space_constraint(x, pltpu.VMEM) for x in (own, other)],
      inner_order, inner_adjoint)
    row = pl.BlockSpec((count, 1, depth, width), lambda s, *_: (0, s * (rows - 1), 0, 0))
    return pl.pallas_call(
        edge_kernel,
        grid_spec=scalars(num_scalar_prefetch=2, grid=(2,), in_specs=[on_chip, on_chip, on_chip, row, row], out_specs=[row, row]),
        out_shape=[jax.ShapeDtypeStruct(order_field.shape, jnp.float32)] * 2,
        input_output_aliases={5: 0, 6: 1},
    )(mobility, flags, *[pltpu.with_memory_space_constraint(x, pltpu.VMEM) for x in (cross, below, above)], order_next, adjoint_order)


def solution(mesh):
    placed = (P("op", "space", None, None), P("op", "space", None, None), P("op"), P("space", None))
    return jax.shard_map(
        local,
        mesh=mesh,
        in_specs=placed,
        out_specs=(P("op", "space", None, None), P("op", "space", None, None)),
        check_vma=False,
    )
```

```python
import jax
import jax.numpy as jnp
from jax import lax
from jax.experimental import pallas as pl
from jax.experimental.pallas import tpu as pltpu
from jax.sharding import PartitionSpec as P


def shift_along(cells, axis, step):
    count = lax.axis_size(axis)
    return lax.ppermute(cells, axis, [(i, (i + step) % count) for i in range(count)])


def stencil(depth, width):
    level = lax.broadcasted_iota(jnp.int32, (depth, width), 0)
    top = level == depth - 1
    bottom = level == 0

    def laplace(centre, beside):
        beside = beside + pltpu.roll(centre, 1, 1) + pltpu.roll(centre, width - 1, 1)
        upper = jnp.where(top, centre, pltpu.roll(centre, depth - 1, 0))
        lower = jnp.where(bottom, centre, pltpu.roll(centre, 1, 0))
        return beside + upper + lower - 6.0 * centre

    return laplace


def inner_kernel(rate_ref, index_ref, labels_ref, order_ref, adjoint_ref, inner_order_ref, inner_adjoint_ref):
    group = order_ref.shape[0]
    for q in range(group):
        inner_one(q, pl.program_id(0) * group + q, rate_ref, index_ref, labels_ref, order_ref, adjoint_ref,
                  inner_order_ref, inner_adjoint_ref)


def inner_one(q, p, rate_ref, index_ref, labels_ref, order_ref, adjoint_ref, inner_order_ref, inner_adjoint_ref):
    rate = 0.1 * rate_ref[p]
    index = index_ref[p]
    _, rows, depth, width = order_ref.shape
    laplace = stencil(depth, width)

    def load(j):
        return order_ref[q, j], rate * adjoint_ref[q, j]

    prev = None
    cur = load(0)
    for j in range(rows):
        nxt = load(j + 1) if j + 1 < rows else None
        o, w = cur
        if prev is None:
            beside = nxt
        elif nxt is None:
            beside = prev
        else:
            beside = (prev[0] + nxt[0], prev[1] + nxt[1])
        sign = jnp.where(labels_ref[j : j + 1, :] != index, 1.0, -1.0)
        inner_order_ref[q, j] = sign * o - 2.0 * (o * o * o) - 0.5 * laplace(o, beside[0])
        inner_adjoint_ref[q, j] = (sign - 6.0 * o * o) * w - 0.5 * laplace(w, beside[1])
        prev, cur = cur, nxt


def final_kernel(rate_ref, order_ref, adjoint_ref, own_ref, other_ref, inner_order_ref, inner_adjoint_ref,
                 order_next_ref, adjoint_order_ref, edge_ref):
    group, rows = order_ref.shape[:2]
    for q in range(group):
        p = pl.program_id(0) * group + q
        final_one(q, p, rate_ref, order_ref, adjoint_ref, own_ref, other_ref,
                  inner_order_ref, inner_adjoint_ref, order_next_ref, adjoint_order_ref)
        for s, r in enumerate((0, rows - 1)):
            edge_ref[s, p] = adjoint_order_ref[q, r]


def final_one(q, p, rate_ref, order_ref, adjoint_ref, own_ref, other_ref, inner_order_ref, inner_adjoint_ref,
              order_next_ref, adjoint_order_ref):
    rate = 0.1 * rate_ref[p]
    rows = order_ref.shape[1]
    for j in range(rows):
        o = order_ref[q, j]
        adj = adjoint_ref[q, j]
        w = rate * adj
        squares = 3.0 * (own_ref[0, j] + other_ref[0, j])
        coupled = 6.0 * (own_ref[1, j] + other_ref[1, j])
        order_next_ref[q, j] = o - rate * (inner_order_ref[q, j] + o * squares)
        adjoint_order_ref[q, j] = adj - ((inner_adjoint_ref[q, j] + w * squares) + o * coupled)


def edge_kernel(rate_ref, below_ref, above_ref, edge_ref, order_next_in, adjoint_order_in, order_next_ref, adjoint_order_ref,
                rows_buf, load_sem, store_sem):
    count, rows = order_next_in.shape[:2]
    loads = [
        pltpu.make_async_copy(order_next_in.at[:, pl.ds(r, 1)], rows_buf.at[0, s], load_sem.at[s])
        for s, r in enumerate((0, rows - 1))
    ]
    for copy in loads:
        copy.start()
    for copy in loads:
        copy.wait()
    for s, halo in enumerate((below_ref, above_ref)):
        for p in range(count):
            rate = 0.1 * rate_ref[p]
            rows_buf[0, s, p, 0] = rows_buf[0, s, p, 0] + (0.5 * rate) * halo[0, p, 0]
            rows_buf[1, s, p, 0] = edge_ref[s, p] + 0.5 * (rate * halo[1, p, 0])
    stores = []
    for a, target in enumerate((order_next_ref, adjoint_order_ref)):
        for s, r in enumerate((0, rows - 1)):
            copy = pltpu.make_async_copy(rows_buf.at[a, s], target.at[:, pl.ds(r, 1)], store_sem.at[a, s])
            copy.start()
            stores.append(copy)
    for copy in stores:
        copy.wait()


def local(order_field, adjoint_next, mobility, labels):
    count, rows, depth, width = order_field.shape
    first = lax.axis_index("op") * count
    indices = first + jnp.arange(count, dtype=jnp.int32)
    rates = mobility[:, None, None, None]
    weighted = 0.1 * rates * adjoint_next
    own = jnp.stack([jnp.sum(order_field * order_field, axis=0), jnp.sum(order_field * weighted, axis=0)])
    other = shift_along(own, "op", 1)
    pair = jnp.stack([order_field, adjoint_next])
    edges = jnp.concatenate([pair[:, :, :1], pair[:, :, -1:]], axis=2)
    edges, own, order_late, adjoint_late = lax.optimization_barrier((edges, own, order_field, adjoint_next))
    below = shift_along(edges[:, :, 1:], "space", 1)
    above = shift_along(edges[:, :, :1], "space", -1)
    scalars = pltpu.PrefetchScalarGridSpec
    group = 4
    block = pl.BlockSpec((group, rows, depth, width), lambda p, *_: (p, 0, 0, 0))
    plane = pl.BlockSpec((rows, width), lambda p, *_: (0, 0))
    inner_order, inner_adjoint = pl.pallas_call(
        inner_kernel,
        grid_spec=scalars(num_scalar_prefetch=2, grid=(count // group,), in_specs=[plane, block, block], out_specs=[block, block]),
        out_shape=[jax.ShapeDtypeStruct(order_field.shape, jnp.float32)] * 2,
    )(mobility, indices, labels, order_late, adjoint_late)
    on_chip = pl.BlockSpec(memory_space=pltpu.VMEM)
    order_next, adjoint_order, edge_rows = pl.pallas_call(
        final_kernel,
        grid_spec=scalars(
            num_scalar_prefetch=1,
            grid=(count // group,),
            in_specs=[block, block, on_chip, on_chip, block, block],
            out_specs=[block, block, on_chip],
        ),
        out_shape=[jax.ShapeDtypeStruct(order_field.shape, jnp.float32)] * 2
        + [pltpu.VMEM((2, count, depth, width), jnp.float32)],
    )(mobility, order_field, adjoint_next, *[pltpu.with_memory_space_constraint(x, pltpu.VMEM) for x in (own, other)],
      inner_order, inner_adjoint)
    anywhere = pl.BlockSpec(memory_space=pl.ANY)
    return pl.pallas_call(
        edge_kernel,
        in_specs=[pl.BlockSpec(memory_space=pltpu.SMEM), on_chip, on_chip, on_chip, anywhere, anywhere],
        out_specs=[anywhere, anywhere],
        out_shape=[jax.ShapeDtypeStruct(order_field.shape, jnp.float32)] * 2,
        scratch_shapes=[
            pltpu.VMEM((2, 2, count, 1, depth, width), jnp.float32),
            pltpu.SemaphoreType.DMA((2,)),
            pltpu.SemaphoreType.DMA((2, 2)),
        ],
        input_output_aliases={4: 0, 5: 1},
    )(mobility, *[pltpu.with_memory_space_constraint(x, pltpu.VMEM) for x in (below, above, edge_rows)], order_next, adjoint_order)


def solution(mesh):
    placed = (P("op", "space", None, None), P("op", "space", None, None), P("op"), P("space", None))
    return jax.shard_map(
        local,
        mesh=mesh,
        in_specs=placed,
        out_specs=(P("op", "space", None, None), P("op", "space", None, None)),
        check_vma=False,
    )
```

```python
import jax
import jax.numpy as jnp
from jax import lax
from jax.experimental import pallas as pl
from jax.experimental.pallas import tpu as pltpu
from jax.sharding import PartitionSpec as P


def shift_along(cells, axis, step):
    count = lax.axis_size(axis)
    return lax.ppermute(cells, axis, [(i, (i + step) % count) for i in range(count)])


def stencil(depth, width):
    level = lax.broadcasted_iota(jnp.int32, (depth, width), 0)
    top = level == depth - 1
    bottom = level == 0

    def laplace(centre, beside):
        beside = beside + pltpu.roll(centre, 1, 1) + pltpu.roll(centre, width - 1, 1)
        upper = jnp.where(top, centre, pltpu.roll(centre, depth - 1, 0))
        lower = jnp.where(bottom, centre, pltpu.roll(centre, 1, 0))
        return beside + upper + lower - 6.0 * centre

    return laplace


def inner_kernel(rate_ref, index_ref, labels_ref, order_ref, adjoint_ref, inner_order_ref, inner_adjoint_ref):
    group = order_ref.shape[0]
    for q in range(group):
        inner_one(q, pl.program_id(0) * group + q, rate_ref, index_ref, labels_ref, order_ref, adjoint_ref,
                  inner_order_ref, inner_adjoint_ref)


def inner_one(q, p, rate_ref, index_ref, labels_ref, order_ref, adjoint_ref, inner_order_ref, inner_adjoint_ref):
    rate = 0.1 * rate_ref[p]
    index = index_ref[p]
    _, rows, depth, width = order_ref.shape
    laplace = stencil(depth, width)

    def load(j):
        return order_ref[q, j], rate * adjoint_ref[q, j]

    prev = None
    cur = load(0)
    for j in range(rows):
        nxt = load(j + 1) if j + 1 < rows else None
        o, w = cur
        if prev is None:
            beside = nxt
        elif nxt is None:
            beside = prev
        else:
            beside = (prev[0] + nxt[0], prev[1] + nxt[1])
        sign = jnp.where(labels_ref[j : j + 1, :] != index, 1.0, -1.0)
        inner_order_ref[q, j] = sign * o - 2.0 * (o * o * o) - 0.5 * laplace(o, beside[0])
        inner_adjoint_ref[q, j] = (sign - 6.0 * o * o) * w - 0.5 * laplace(w, beside[1])
        prev, cur = cur, nxt


def final_kernel(rate_ref, order_ref, adjoint_ref, own_ref, other_ref, inner_order_ref, inner_adjoint_ref,
                 order_next_ref, adjoint_order_ref):
    group, rows = order_ref.shape[:2]
    for q in range(group):
        final_one(q, pl.program_id(0) * group + q, rate_ref, order_ref, adjoint_ref, own_ref, other_ref,
                  inner_order_ref, inner_adjoint_ref, order_next_ref, adjoint_order_ref)


def final_one(q, p, rate_ref, order_ref, adjoint_ref, own_ref, other_ref, inner_order_ref, inner_adjoint_ref,
              order_next_ref, adjoint_order_ref):
    rate = 0.1 * rate_ref[p]
    rows = order_ref.shape[1]
    for j in range(rows):
        o = order_ref[q, j]
        adj = adjoint_ref[q, j]
        w = rate * adj
        squares = 3.0 * (own_ref[0, j] + other_ref[0, j])
        coupled = 6.0 * (own_ref[1, j] + other_ref[1, j])
        order_next_ref[q, j] = o - rate * (inner_order_ref[q, j] + o * squares)
        adjoint_order_ref[q, j] = adj - ((inner_adjoint_ref[q, j] + w * squares) + o * coupled)


def edge_kernel(rate_ref, below_ref, above_ref, order_next_in, adjoint_order_in, order_next_ref, adjoint_order_ref):
    side = pl.program_id(0)
    count = order_next_in.shape[0]
    for p in range(count):
        rate = 0.1 * rate_ref[p]
        order_row = jnp.where(side == 0, below_ref[0, p, 0], above_ref[0, p, 0])
        adjoint_row = jnp.where(side == 0, below_ref[1, p, 0], above_ref[1, p, 0])
        order_next_ref[p, 0] = order_next_in[p, 0] + (0.5 * rate) * order_row
        adjoint_order_ref[p, 0] = adjoint_order_in[p, 0] + 0.5 * (rate * adjoint_row)


def local(order_field, adjoint_next, mobility, labels):
    count, rows, depth, width = order_field.shape
    first = lax.axis_index("op") * count
    indices = first + jnp.arange(count, dtype=jnp.int32)
    scale = 0.1 * mobility
    squares = order_field[0] * order_field[0]
    coupled = order_field[0] * (scale[0] * adjoint_next[0])
    for p in range(1, count):
        squares = squares + order_field[p] * order_field[p]
        coupled = coupled + order_field[p] * (scale[p] * adjoint_next[p])
    own = jnp.stack([squares, coupled])
    other = shift_along(own, "op", 1)
    pair = jnp.stack([order_field, adjoint_next])
    edges = jnp.concatenate([pair[:, :, :1], pair[:, :, -1:]], axis=2)
    edges, own, order_late, adjoint_late = lax.optimization_barrier((edges, own, order_field, adjoint_next))
    below = shift_along(edges[:, :, 1:], "space", 1)
    above = shift_along(edges[:, :, :1], "space", -1)
    scalars = pltpu.PrefetchScalarGridSpec
    group = 4
    block = pl.BlockSpec((group, rows, depth, width), lambda p, *_: (p, 0, 0, 0))
    plane = pl.BlockSpec((rows, width), lambda p, *_: (0, 0))
    inner_order, inner_adjoint = pl.pallas_call(
        inner_kernel,
        grid_spec=scalars(num_scalar_prefetch=2, grid=(count // group,), in_specs=[plane, block, block], out_specs=[block, block]),
        out_shape=[jax.ShapeDtypeStruct(order_field.shape, jnp.float32)] * 2,
    )(mobility, indices, labels, order_late, adjoint_late)
    on_chip = pl.BlockSpec(memory_space=pltpu.VMEM)
    order_next, adjoint_order = pl.pallas_call(
        final_kernel,
        grid_spec=scalars(num_scalar_prefetch=1, grid=(count // group,), in_specs=[block, block, on_chip, on_chip, block, block], out_specs=[block, block]),
        out_shape=[jax.ShapeDtypeStruct(order_field.shape, jnp.float32)] * 2,
    )(mobility, order_field, adjoint_next, *[pltpu.with_memory_space_constraint(x, pltpu.VMEM) for x in (own, other)],
      inner_order, inner_adjoint)
    row = pl.BlockSpec((count, 1, depth, width), lambda s, *_: (0, s * (rows - 1), 0, 0))
    return pl.pallas_call(
        edge_kernel,
        grid_spec=scalars(num_scalar_prefetch=1, grid=(2,), in_specs=[on_chip, on_chip, row, row], out_specs=[row, row]),
        out_shape=[jax.ShapeDtypeStruct(order_field.shape, jnp.float32)] * 2,
        input_output_aliases={3: 0, 4: 1},
    )(mobility, *[pltpu.with_memory_space_constraint(x, pltpu.VMEM) for x in (below, above)], order_next, adjoint_order)


def solution(mesh):
    placed = (P("op", "space", None, None), P("op", "space", None, None), P("op"), P("space", None))
    return jax.shard_map(
        local,
        mesh=mesh,
        in_specs=placed,
        out_specs=(P("op", "space", None, None), P("op", "space", None, None)),
        check_vma=False,
    )
```

```python
import jax
import jax.numpy as jnp
from jax import lax
from jax.experimental import pallas as pl
from jax.experimental.pallas import tpu as pltpu
from jax.sharding import PartitionSpec as P


def shift_along(cells, axis, step):
    count = lax.axis_size(axis)
    return lax.ppermute(cells, axis, [(i, (i + step) % count) for i in range(count)])


def stencil(depth, width):
    level = lax.broadcasted_iota(jnp.int32, (depth, width), 0)
    top = level == depth - 1
    bottom = level == 0

    def laplace(centre, beside):
        beside = beside + pltpu.roll(centre, 1, 1) + pltpu.roll(centre, width - 1, 1)
        upper = jnp.where(top, centre, pltpu.roll(centre, depth - 1, 0))
        lower = jnp.where(bottom, centre, pltpu.roll(centre, 1, 0))
        return beside + upper + lower - 6.0 * centre

    return laplace


def inner_kernel(rate_ref, index_ref, labels_ref, order_ref, adjoint_ref, inner_ref):
    group = order_ref.shape[0]
    for q in range(group):
        inner_one(q, pl.program_id(0) * group + q, rate_ref, index_ref, labels_ref, order_ref, adjoint_ref,
                  inner_ref.at[:, 0], inner_ref.at[:, 1])


def inner_one(q, p, rate_ref, index_ref, labels_ref, order_ref, adjoint_ref, inner_order_ref, inner_adjoint_ref):
    rate = 0.1 * rate_ref[p]
    index = index_ref[p]
    _, rows, depth, width = order_ref.shape
    laplace = stencil(depth, width)

    def load(j):
        return order_ref[q, j], rate * adjoint_ref[q, j]

    prev = None
    cur = load(0)
    for j in range(rows):
        nxt = load(j + 1) if j + 1 < rows else None
        o, w = cur
        if prev is None:
            beside = nxt
        elif nxt is None:
            beside = prev
        else:
            beside = (prev[0] + nxt[0], prev[1] + nxt[1])
        sign = jnp.where(labels_ref[j : j + 1, :] != index, 1.0, -1.0)
        inner_order_ref[q, j] = sign * o - 2.0 * (o * o * o) - 0.5 * laplace(o, beside[0])
        inner_adjoint_ref[q, j] = (sign - 6.0 * o * o) * w - 0.5 * laplace(w, beside[1])
        prev, cur = cur, nxt


def final_kernel(rate_ref, order_ref, adjoint_ref, own_ref, other_ref, inner_ref, order_next_ref, adjoint_order_ref):
    group, rows = order_ref.shape[:2]
    for q in range(group):
        final_one(q, pl.program_id(0) * group + q, rate_ref, order_ref, adjoint_ref, own_ref, other_ref,
                  inner_ref.at[:, 0], inner_ref.at[:, 1], order_next_ref, adjoint_order_ref)


def final_one(q, p, rate_ref, order_ref, adjoint_ref, own_ref, other_ref, inner_order_ref, inner_adjoint_ref,
              order_next_ref, adjoint_order_ref):
    rate = 0.1 * rate_ref[p]
    rows = order_ref.shape[1]
    for j in range(rows):
        o = order_ref[q, j]
        adj = adjoint_ref[q, j]
        w = rate * adj
        squares = 3.0 * (own_ref[0, j] + other_ref[0, j])
        coupled = 6.0 * (own_ref[1, j] + other_ref[1, j])
        order_next_ref[q, j] = o - rate * (inner_order_ref[q, j] + o * squares)
        adjoint_order_ref[q, j] = adj - ((inner_adjoint_ref[q, j] + w * squares) + o * coupled)


def edge_kernel(rate_ref, below_ref, above_ref, order_next_in, adjoint_order_in, order_next_ref, adjoint_order_ref):
    side = pl.program_id(0)
    count = order_next_in.shape[0]
    for p in range(count):
        rate = 0.1 * rate_ref[p]
        order_row = jnp.where(side == 0, below_ref[0, p, 0], above_ref[0, p, 0])
        adjoint_row = jnp.where(side == 0, below_ref[1, p, 0], above_ref[1, p, 0])
        order_next_ref[p, 0] = order_next_in[p, 0] + (0.5 * rate) * order_row
        adjoint_order_ref[p, 0] = adjoint_order_in[p, 0] + 0.5 * (rate * adjoint_row)


def local(order_field, adjoint_next, mobility, labels):
    count, rows, depth, width = order_field.shape
    first = lax.axis_index("op") * count
    indices = first + jnp.arange(count, dtype=jnp.int32)
    rates = mobility[:, None, None, None]
    weighted = 0.1 * rates * adjoint_next
    own = jnp.stack([jnp.sum(order_field * order_field, axis=0), jnp.sum(order_field * weighted, axis=0)])
    other = shift_along(own, "op", 1)
    pair = jnp.stack([order_field, adjoint_next])
    edges = jnp.concatenate([pair[:, :, :1], pair[:, :, -1:]], axis=2)
    edges, own, order_late, adjoint_late = lax.optimization_barrier((edges, own, order_field, adjoint_next))
    below = shift_along(edges[:, :, 1:], "space", 1)
    above = shift_along(edges[:, :, :1], "space", -1)
    scalars = pltpu.PrefetchScalarGridSpec
    group = 4
    block = pl.BlockSpec((group, rows, depth, width), lambda p, *_: (p, 0, 0, 0))
    plane = pl.BlockSpec((rows, width), lambda p, *_: (0, 0))
    both = pl.BlockSpec((group, 2, rows, depth, width), lambda p, *_: (p, 0, 0, 0, 0))
    inner = pl.pallas_call(
        inner_kernel,
        grid_spec=scalars(num_scalar_prefetch=2, grid=(count // group,), in_specs=[plane, block, block], out_specs=both),
        out_shape=jax.ShapeDtypeStruct((count, 2, rows, depth, width), jnp.float32),
    )(mobility, indices, labels, order_late, adjoint_late)
    on_chip = pl.BlockSpec(memory_space=pltpu.VMEM)
    order_next, adjoint_order = pl.pallas_call(
        final_kernel,
        grid_spec=scalars(num_scalar_prefetch=1, grid=(count // group,), in_specs=[block, block, on_chip, on_chip, both], out_specs=[block, block]),
        out_shape=[jax.ShapeDtypeStruct(order_field.shape, jnp.float32)] * 2,
    )(mobility, order_field, adjoint_next, *[pltpu.with_memory_space_constraint(x, pltpu.VMEM) for x in (own, other)], inner)
    row = pl.BlockSpec((count, 1, depth, width), lambda s, *_: (0, s * (rows - 1), 0, 0))
    return pl.pallas_call(
        edge_kernel,
        grid_spec=scalars(num_scalar_prefetch=1, grid=(2,), in_specs=[on_chip, on_chip, row, row], out_specs=[row, row]),
        out_shape=[jax.ShapeDtypeStruct(order_field.shape, jnp.float32)] * 2,
        input_output_aliases={3: 0, 4: 1},
    )(mobility, *[pltpu.with_memory_space_constraint(x, pltpu.VMEM) for x in (below, above)], order_next, adjoint_order)


def solution(mesh):
    placed = (P("op", "space", None, None), P("op", "space", None, None), P("op"), P("space", None))
    return jax.shard_map(
        local,
        mesh=mesh,
        in_specs=placed,
        out_specs=(P("op", "space", None, None), P("op", "space", None, None)),
        check_vma=False,
    )
```

```python
import jax
import jax.numpy as jnp
from jax import lax
from jax.experimental import pallas as pl
from jax.experimental.pallas import tpu as pltpu
from jax.sharding import PartitionSpec as P


def shift_along(cells, axis, step):
    count = lax.axis_size(axis)
    return lax.ppermute(cells, axis, [(i, (i + step) % count) for i in range(count)])


def stencil(depth, width):
    level = lax.broadcasted_iota(jnp.int32, (depth, width), 0)
    top = level == depth - 1
    bottom = level == 0

    def laplace(centre, beside):
        beside = beside + pltpu.roll(centre, 1, 1) + pltpu.roll(centre, width - 1, 1)
        upper = jnp.where(top, centre, pltpu.roll(centre, depth - 1, 0))
        lower = jnp.where(bottom, centre, pltpu.roll(centre, 1, 0))
        return beside + upper + lower - 6.0 * centre

    return laplace


def inner_kernel(rate_ref, index_ref, labels_ref, order_ref, adjoint_ref, inner_order_ref, inner_adjoint_ref):
    group = order_ref.shape[0]
    for q in range(group):
        inner_one(q, pl.program_id(0) * group + q, rate_ref, index_ref, labels_ref, order_ref, adjoint_ref,
                  inner_order_ref, inner_adjoint_ref)


def inner_one(q, p, rate_ref, index_ref, labels_ref, order_ref, adjoint_ref, inner_order_ref, inner_adjoint_ref):
    rate = 0.1 * rate_ref[p]
    index = index_ref[p]
    _, rows, depth, width = order_ref.shape
    laplace = stencil(depth, width)

    def load(j):
        return order_ref[q, j], rate * adjoint_ref[q, j]

    prev = None
    cur = load(0)
    for j in range(rows):
        nxt = load(j + 1) if j + 1 < rows else None
        o, w = cur
        if prev is None:
            beside = nxt
        elif nxt is None:
            beside = prev
        else:
            beside = (prev[0] + nxt[0], prev[1] + nxt[1])
        sign = jnp.where(labels_ref[j : j + 1, :] != index, 1.0, -1.0)
        inner_order_ref[q, j] = sign * o - 2.0 * (o * o * o) - 0.5 * laplace(o, beside[0])
        inner_adjoint_ref[q, j] = (sign - 6.0 * o * o) * w - 0.5 * laplace(w, beside[1])
        prev, cur = cur, nxt


def final_kernel(rate_ref, order_ref, adjoint_ref, own_ref, other_ref, inner_order_ref, inner_adjoint_ref,
                 order_next_ref, adjoint_order_ref):
    group, rows = order_ref.shape[:2]
    for q in range(group):
        final_one(q, pl.program_id(0) * group + q, rate_ref, order_ref, adjoint_ref, own_ref, other_ref,
                  inner_order_ref, inner_adjoint_ref, order_next_ref, adjoint_order_ref)


def final_one(q, p, rate_ref, order_ref, adjoint_ref, own_ref, other_ref, inner_order_ref, inner_adjoint_ref,
              order_next_ref, adjoint_order_ref):
    rate = 0.1 * rate_ref[p]
    rows = order_ref.shape[1]
    for j in range(rows):
        o = order_ref[q, j]
        adj = adjoint_ref[q, j]
        w = rate * adj
        squares = 3.0 * (own_ref[0, j] + other_ref[0, j])
        coupled = 6.0 * (own_ref[1, j] + other_ref[1, j])
        order_next_ref[q, j] = o - rate * (inner_order_ref[q, j] + o * squares)
        adjoint_order_ref[q, j] = adj - ((inner_adjoint_ref[q, j] + w * squares) + o * coupled)


def edge_kernel(rate_ref, below_ref, above_ref, order_next_in, adjoint_order_in, order_next_ref, adjoint_order_ref):
    side = pl.program_id(0)
    count = order_next_in.shape[0]
    for p in range(count):
        rate = 0.1 * rate_ref[p]
        order_row = jnp.where(side == 0, below_ref[0, p, 0], above_ref[0, p, 0])
        adjoint_row = jnp.where(side == 0, below_ref[1, p, 0], above_ref[1, p, 0])
        order_next_ref[p, 0] = order_next_in[p, 0] + (0.5 * rate) * order_row
        adjoint_order_ref[p, 0] = adjoint_order_in[p, 0] + 0.5 * (rate * adjoint_row)


def local(order_field, adjoint_next, mobility, labels):
    count, rows, depth, width = order_field.shape
    first = lax.axis_index("op") * count
    indices = first + jnp.arange(count, dtype=jnp.int32)
    rates = mobility[:, None, None, None]
    own = jnp.stack([jnp.sum(order_field * order_field, axis=0), 0.1 * jnp.sum(order_field * (rates * adjoint_next), axis=0)])
    other = shift_along(own, "op", 1)
    pair = jnp.stack([order_field, adjoint_next])
    edges = jnp.concatenate([pair[:, :, :1], pair[:, :, -1:]], axis=2)
    edges, own, order_late, adjoint_late = lax.optimization_barrier((edges, own, order_field, adjoint_next))
    below = shift_along(edges[:, :, 1:], "space", 1)
    above = shift_along(edges[:, :, :1], "space", -1)
    scalars = pltpu.PrefetchScalarGridSpec
    group = 4
    block = pl.BlockSpec((group, rows, depth, width), lambda p, *_: (p, 0, 0, 0))
    plane = pl.BlockSpec((rows, width), lambda p, *_: (0, 0))
    inner_order, inner_adjoint = pl.pallas_call(
        inner_kernel,
        grid_spec=scalars(num_scalar_prefetch=2, grid=(count // group,), in_specs=[plane, block, block], out_specs=[block, block]),
        out_shape=[jax.ShapeDtypeStruct(order_field.shape, jnp.float32)] * 2,
    )(mobility, indices, labels, order_late, adjoint_late)
    on_chip = pl.BlockSpec(memory_space=pltpu.VMEM)
    order_next, adjoint_order = pl.pallas_call(
        final_kernel,
        grid_spec=scalars(num_scalar_prefetch=1, grid=(count // group,), in_specs=[block, block, on_chip, on_chip, block, block], out_specs=[block, block]),
        out_shape=[jax.ShapeDtypeStruct(order_field.shape, jnp.float32)] * 2,
    )(mobility, order_field, adjoint_next, *[pltpu.with_memory_space_constraint(x, pltpu.VMEM) for x in (own, other)],
      inner_order, inner_adjoint)
    row = pl.BlockSpec((count, 1, depth, width), lambda s, *_: (0, s * (rows - 1), 0, 0))
    return pl.pallas_call(
        edge_kernel,
        grid_spec=scalars(num_scalar_prefetch=1, grid=(2,), in_specs=[on_chip, on_chip, row, row], out_specs=[row, row]),
        out_shape=[jax.ShapeDtypeStruct(order_field.shape, jnp.float32)] * 2,
        input_output_aliases={3: 0, 4: 1},
    )(mobility, *[pltpu.with_memory_space_constraint(x, pltpu.VMEM) for x in (below, above)], order_next, adjoint_order)


def solution(mesh):
    placed = (P("op", "space", None, None), P("op", "space", None, None), P("op"), P("space", None))
    return jax.shard_map(
        local,
        mesh=mesh,
        in_specs=placed,
        out_specs=(P("op", "space", None, None), P("op", "space", None, None)),
        check_vma=False,
    )
```

```python
import jax
import jax.numpy as jnp
from jax import lax
from jax.experimental import pallas as pl
from jax.experimental.pallas import tpu as pltpu
from jax.sharding import PartitionSpec as P


def shift_along(cells, axis, step):
    count = lax.axis_size(axis)
    return lax.ppermute(cells, axis, [(i, (i + step) % count) for i in range(count)])


def stencil(depth, width):
    level = lax.broadcasted_iota(jnp.int32, (depth, width), 0)
    top = level == depth - 1
    bottom = level == 0

    def laplace(centre, beside):
        beside = beside + pltpu.roll(centre, 1, 1) + pltpu.roll(centre, width - 1, 1)
        upper = jnp.where(top, centre, pltpu.roll(centre, depth - 1, 0))
        lower = jnp.where(bottom, centre, pltpu.roll(centre, 1, 0))
        return beside + upper + lower - 6.0 * centre

    return laplace


def inner_kernel(rate_ref, index_ref, labels_ref, order_ref, adjoint_ref, inner_ref):
    group = order_ref.shape[0]
    for q in range(group):
        inner_one(q, pl.program_id(0) * group + q, rate_ref, index_ref, labels_ref, order_ref, adjoint_ref,
                  inner_ref.at[:, 0], inner_ref.at[:, 1])


def inner_one(q, p, rate_ref, index_ref, labels_ref, order_ref, adjoint_ref, inner_order_ref, inner_adjoint_ref):
    rate = 0.1 * rate_ref[p]
    index = index_ref[p]
    _, rows, depth, width = order_ref.shape
    laplace = stencil(depth, width)

    def load(j):
        return order_ref[q, j], rate * adjoint_ref[q, j]

    prev = None
    cur = load(0)
    for j in range(rows):
        nxt = load(j + 1) if j + 1 < rows else None
        o, w = cur
        if prev is None:
            beside = nxt
        elif nxt is None:
            beside = prev
        else:
            beside = (prev[0] + nxt[0], prev[1] + nxt[1])
        sign = jnp.where(labels_ref[j : j + 1, :] != index, 1.0, -1.0)
        inner_order_ref[q, j] = sign * o - 2.0 * (o * o * o) - 0.5 * laplace(o, beside[0])
        inner_adjoint_ref[q, j] = (sign - 6.0 * o * o) * w - 0.5 * laplace(w, beside[1])
        prev, cur = cur, nxt


def final_kernel(rate_ref, order_ref, adjoint_ref, own_ref, other_ref, inner_ref, order_next_ref, adjoint_order_ref):
    group, rows = order_ref.shape[:2]
    for q in range(group):
        final_one(q, pl.program_id(0) * group + q, rate_ref, order_ref, adjoint_ref, own_ref, other_ref,
                  inner_ref.at[:, 0], inner_ref.at[:, 1], order_next_ref, adjoint_order_ref)


def final_one(q, p, rate_ref, order_ref, adjoint_ref, own_ref, other_ref, inner_order_ref, inner_adjoint_ref,
              order_next_ref, adjoint_order_ref):
    rate = 0.1 * rate_ref[p]
    rows = order_ref.shape[1]
    for j in range(rows):
        o = order_ref[q, j]
        adj = adjoint_ref[q, j]
        w = rate * adj
        squares = 3.0 * (own_ref[0, j] + other_ref[0, j])
        coupled = 6.0 * (own_ref[1, j] + other_ref[1, j])
        order_next_ref[q, j] = o - rate * (inner_order_ref[q, j] + o * squares)
        adjoint_order_ref[q, j] = adj - ((inner_adjoint_ref[q, j] + w * squares) + o * coupled)


def edge_kernel(rate_ref, below_ref, above_ref, order_next_in, adjoint_order_in, order_next_ref, adjoint_order_ref):
    side = pl.program_id(0)
    count = order_next_in.shape[0]
    for p in range(count):
        rate = 0.1 * rate_ref[p]
        order_row = jnp.where(side == 0, below_ref[0, p, 0], above_ref[0, p, 0])
        adjoint_row = jnp.where(side == 0, below_ref[1, p, 0], above_ref[1, p, 0])
        order_next_ref[p, 0] = order_next_in[p, 0] + (0.5 * rate) * order_row
        adjoint_order_ref[p, 0] = adjoint_order_in[p, 0] + 0.5 * (rate * adjoint_row)


def local(order_field, adjoint_next, mobility, labels):
    count, rows, depth, width = order_field.shape
    first = lax.axis_index("op") * count
    indices = first + jnp.arange(count, dtype=jnp.int32)
    rates = mobility[:, None, None, None]
    own = jnp.stack([jnp.sum(order_field * order_field, axis=0), 0.1 * jnp.sum(order_field * (rates * adjoint_next), axis=0)])
    other = shift_along(own, "op", 1)
    pair = jnp.stack([order_field, adjoint_next])
    edges = jnp.concatenate([pair[:, :, :1], pair[:, :, -1:]], axis=2)
    edges, own, order_late, adjoint_late = lax.optimization_barrier((edges, own, order_field, adjoint_next))
    below = shift_along(edges[:, :, 1:], "space", 1)
    above = shift_along(edges[:, :, :1], "space", -1)
    scalars = pltpu.PrefetchScalarGridSpec
    group = 4
    block = pl.BlockSpec((group, rows, depth, width), lambda p, *_: (p, 0, 0, 0))
    plane = pl.BlockSpec((rows, width), lambda p, *_: (0, 0))
    both = pl.BlockSpec((group, 2, rows, depth, width), lambda p, *_: (p, 0, 0, 0, 0))
    inner = pl.pallas_call(
        inner_kernel,
        grid_spec=scalars(num_scalar_prefetch=2, grid=(count // group,), in_specs=[plane, block, block], out_specs=both),
        out_shape=jax.ShapeDtypeStruct((count, 2, rows, depth, width), jnp.float32),
    )(mobility, indices, labels, order_late, adjoint_late)
    on_chip = pl.BlockSpec(memory_space=pltpu.VMEM)
    order_next, adjoint_order = pl.pallas_call(
        final_kernel,
        grid_spec=scalars(num_scalar_prefetch=1, grid=(count // group,), in_specs=[block, block, on_chip, on_chip, both], out_specs=[block, block]),
        out_shape=[jax.ShapeDtypeStruct(order_field.shape, jnp.float32)] * 2,
    )(mobility, order_field, adjoint_next, *[pltpu.with_memory_space_constraint(x, pltpu.VMEM) for x in (own, other)], inner)
    row = pl.BlockSpec((count, 1, depth, width), lambda s, *_: (0, s * (rows - 1), 0, 0))
    return pl.pallas_call(
        edge_kernel,
        grid_spec=scalars(num_scalar_prefetch=1, grid=(2,), in_specs=[on_chip, on_chip, row, row], out_specs=[row, row]),
        out_shape=[jax.ShapeDtypeStruct(order_field.shape, jnp.float32)] * 2,
        input_output_aliases={3: 0, 4: 1},
    )(mobility, *[pltpu.with_memory_space_constraint(x, pltpu.VMEM) for x in (below, above)], order_next, adjoint_order)


def solution(mesh):
    placed = (P("op", "space", None, None), P("op", "space", None, None), P("op"), P("space", None))
    return jax.shard_map(
        local,
        mesh=mesh,
        in_specs=placed,
        out_specs=(P("op", "space", None, None), P("op", "space", None, None)),
        check_vma=False,
    )
```
